256 devices in a mesh: group: 16 (over y, x), dp: 8 (over z), space: 2 (over core).
Axes of the slice: x: 4, y: 4, z: 8, core: 2. Of those that a mesh axis runs over, the one named last changes fastest.
Arguments:
- video: bfloat16 [8, 32, 16, 64, 256], P('dp', 'group', 'space'), may hold values from -6 to 6
- cotangent: bfloat16 [8, 32, 16, 64, 256], P('dp', 'group', 'space'), may hold values from -6 to 6
- weight: bfloat16 [6912, 256], replicated, may hold values from -0.078125 to 0.078125
- clip_id: int32 [8, 32], P('dp', 'group'), may hold values from 0 to 3, never falling along the last dimension, each value on 1 to 16 neighbouring positions
Outputs:
- activation: bfloat16 [8, 32, 16, 64, 256], P('dp', 'group', 'space')
- grad_video: bfloat16 [8, 32, 16, 64, 256], P('dp', 'group', 'space')
- grad_weight: float32 [27, 65536], P(None, ('group', 'dp', 'space'))
The draws below stay inside these ranges and needn't reach their ends.
Inputs may be any that keep to these rules, and one draw needn't show every extreme that they name: `clip_id`: clip numbers never fall along a stream's frames; every clip spans at most 16 frames and one spans exactly that many.
All inputs are finite; a program needn't handle non-finite values.
Results may differ from the reference program's by a relative error of at most 0.0053.
Values may be sent and summed in bfloat16 or wider, within the bound.
No kernel may reach another device: no remote copies, remote signals or barrier semaphores. Data moves between devices by JAX's collectives and lax.ppermute only.
A program may use at most 128 MiB of HBM per device.

```python
import math
from functools import partial
import jax
import jax.numpy as jnp
import numpy as np
from jax import lax

C = 256
COLS = 64
FRAMES = 32
ROWS = 16
STREAMS = 8


def steps_of(own_key, extent, split, least, largest):
    loudness = 1.0
    for axis_at, parts in split:
        steps = jax.random.uniform(jax.random.fold_in(jax.random.fold_in(own_key, 6), axis_at), (parts,), jnp.float32, least / len(split), largest / len(split))
        loudness = loudness * jnp.repeat(jnp.exp(steps), extent[axis_at] // parts).reshape((-1,) + (1,) * (len(extent) - 1 - axis_at))
    return loudness


def split_up(amount, total, reach, slope):
    loads = [(1 << 20) // math.isqrt(grade ** slope) + 1 for grade in range(2, amount + 1)]
    surplus, counts = total - reach - (amount - 1), [1] * (amount - 1)
    while surplus > 0:
        candidates = [i for i in range(amount - 1) if counts[i] < reach]
        whole, remaining = sum([loads[i] for i in candidates]), surplus
        for i in candidates:
            addition = min(reach - counts[i], max(1, remaining * loads[i] // whole), surplus)
            counts[i] = counts[i] + addition
            surplus = surplus - addition
    return np.array([reach] + counts)


def ragged_sizes(own_key, amount, total, reach, skew):
    if amount == 2:
        one = jax.random.randint(own_key, (), max(1, total - reach), min(reach, total - 1) + 1)
        return jnp.stack([one, total - one])
    sizes = jnp.asarray(split_up(amount, total, reach, skew), jnp.int32)
    couples = (amount - 1) // 2
    source_of, sink = sizes[1:1 + 2 * couples:2], sizes[2:2 + 2 * couples:2]
    room = jnp.minimum(source_of - 1, reach - sink)
    passed = jax.random.randint(jax.random.fold_in(own_key, 1), (couples,), 0, 1 << 20) % (room + 1)
    sizes = sizes.at[1:1 + 2 * couples:2].set(source_of - passed).at[2:2 + 2 * couples:2].set(sink + passed)
    return sizes[jax.random.permutation(jax.random.fold_in(own_key, 2), amount)]


def centred(rng, extent, spread, limit, pieces=(), kind=jnp.bfloat16):
    drawn = jax.random.normal(rng, extent, jnp.float32) * spread
    if len(pieces) > 0:
        drawn = steps_of(rng, extent, pieces, -0.22, 0.18) * drawn
    return jnp.clip(drawn, min=-limit, max=limit).astype(kind)


def setup_inputs(seed: int = 0) -> dict:
    streams_of = jax.random.split(jax.random.key(seed), 5)
    return {
        "video": centred(streams_of[0], (STREAMS, FRAMES, ROWS, COLS, C), 1.0, 6.0, ((0, 8), (1, 16), (2, 2))),
        "cotangent": centred(streams_of[1], (STREAMS, FRAMES, ROWS, COLS, C), 1.0, 6.0, ((0, 8), (1, 16), (2, 2))),
        "weight": centred(streams_of[2], (27 * C, C), (27 * C) ** -0.5, 0.078125),
        "clip_id": jax.vmap(lambda own: jnp.searchsorted(jnp.cumsum(ragged_sizes(own, 4, FRAMES, FRAMES // 2, 0)), jnp.arange(FRAMES), side="right"))(jax.random.split(streams_of[3], STREAMS)).reshape((STREAMS, FRAMES)).astype(jnp.int32),
    }


def one_stream(weight, carry, items):
    video_s, cotangent_s, ids = items
    frames, rows, cols, chans = video_s.shape
    index = jnp.arange(frames, dtype=jnp.int32)
    previous = jnp.concatenate([jnp.full((1,), -1, jnp.int32), ids[:-1]])
    boundary = ids != previous
    position = index - lax.cummax(jnp.where(boundary, index, 0), axis=0)
    omega = 0.37 * ((jnp.arange(chans) % 8) + 1).astype(jnp.float32)
    embed = jnp.sin(position.astype(jnp.float32)[:, None] * omega[None, :])
    shifted = (video_s.astype(jnp.float32) + embed[:, None, None, :]).astype(jnp.bfloat16)
    extended = jnp.concatenate([jnp.full((2,), -1, jnp.int32), ids])
    masks = [(extended[2 - k:2 - k + frames] == ids).astype(jnp.float32) for k in range(3)]
    padded = jnp.pad(shifted, ((2, 0), (1, 1), (1, 1), (0, 0)))
    stacked = jnp.concatenate([padded[:, :, b:b + cols] for b in range(3)], axis=3)
    taps = weight.reshape(3, 3, 3 * chans, chans)
    pre = jnp.zeros((frames, rows, cols, chans), jnp.float32)
    for k in range(3):
        part = jnp.zeros((frames, rows, cols, chans), jnp.float32)
        for a in range(3):
            block = stacked[2 - k:2 - k + frames, a:a + rows].reshape(-1, 3 * chans)
            part = part + jnp.dot(block, taps[k, a], preferred_element_type=jnp.float32).reshape(frames, rows, cols, chans)
        pre = pre + part * masks[k][:, None, None, None]
    sigma = jax.nn.sigmoid(pre)
    activation = (pre * sigma).astype(jnp.bfloat16)
    delta = (cotangent_s.astype(jnp.float32) * sigma * (1.0 + pre * (1.0 - sigma))).astype(jnp.bfloat16)
    back = weight.reshape(3, 3, 3, chans, chans).transpose(0, 1, 2, 4, 3).reshape(3, 3, 3 * chans, chans)
    gpad = jnp.pad(delta, ((0, 2), (1, 1), (1, 1), (0, 0)))
    gstack = jnp.concatenate([gpad[:, :, 2 - b:2 - b + cols] for b in range(3)], axis=3)
    grad = jnp.zeros((frames, rows, cols, chans), jnp.float32)
    for k in range(3):
        ahead = jnp.concatenate([masks[k], jnp.zeros((2,), jnp.float32)])[k:k + frames]
        part = jnp.zeros((frames, rows, cols, chans), jnp.float32)
        for a in range(3):
            block = gstack[k:k + frames, 2 - a:2 - a + rows].reshape(-1, 3 * chans)
            part = part + jnp.dot(block, back[k, a], preferred_element_type=jnp.float32).reshape(frames, rows, cols, chans)
        grad = grad + part * ahead[:, None, None, None]
    terms = []
    for k in range(3):
        masked = (delta * masks[k].astype(jnp.bfloat16)[:, None, None, None]).reshape(-1, chans)
        for a in range(3):
            block = stacked[2 - k:2 - k + frames, a:a + rows].reshape(-1, 3 * chans)
            terms.append(jnp.dot(block.T, masked, preferred_element_type=jnp.float32))
    total = jnp.stack(terms).reshape(27, chans * chans)
    return carry + total, (activation, grad.astype(jnp.bfloat16))


def reference(video, cotangent, weight, clip_id):
    chans = video.shape[-1]
    start = jnp.zeros((27, chans * chans), jnp.float32)
    total, outputs = lax.scan(partial(one_stream, weight), start, (video, cotangent, clip_id))
    return outputs[0], outputs[1], total
```

```python
import jax
import jax.numpy as jnp
from jax import lax
from jax.sharding import PartitionSpec as P

STAGED = True


def passed_along(value, axis, by):
    length = lax.axis_size(axis)
    pairs = [(i, i + by) for i in range(length) if 0 <= i + by < length]
    return lax.ppermute(value, axis, pairs)


def row_halo(block, axis, dim):
    count = lax.axis_size(axis)
    forward = [(i, i + 1) for i in range(count - 1)]
    backward = [(target, source) for source, target in forward]
    low = lax.ppermute(
        lax.slice_in_dim(block, block.shape[dim] - 1, None, axis=dim), axis, forward
    )
    high = lax.ppermute(lax.slice_in_dim(block, 0, 1, axis=dim), axis, backward)
    return jnp.concatenate([low, block, high], axis=dim)


def clip_tables(clip_id, frames):
    ids = lax.all_gather(clip_id, "group", axis=1, tiled=True)
    total = ids.shape[1]
    index = jnp.arange(total, dtype=jnp.int32)[None, :]
    prev = jnp.concatenate([jnp.full_like(ids[:, :1], -1), ids[:, :-1]], axis=1)
    boundary = ids != prev
    start = lax.cummax(jnp.where(boundary, index, 0), axis=1)
    position = index - start
    ext = jnp.concatenate([jnp.full_like(ids[:, :2], -1), ids], axis=1)
    same = jnp.stack([ext[:, 2 - k : 2 - k + total] == ids for k in range(3)], axis=0)
    first = lax.axis_index("group") * frames
    pos_pad = jnp.concatenate([jnp.zeros_like(position[:, :2]), position], axis=1)
    pos_wide = lax.dynamic_slice_in_dim(pos_pad, first, frames + 2, axis=1)
    same_pad = jnp.concatenate([same, jnp.zeros_like(same[:, :, :2])], axis=2)
    own = lax.dynamic_slice_in_dim(same_pad, first, frames + 2, axis=2)
    fwd = own[:, :, :frames]
    bwd = jnp.stack([own[k, :, k : k + frames] for k in range(3)], axis=0)
    return pos_wide, fwd, bwd


def local(video, cotangent, weight, clip_id):
    frames = video.shape[1]
    rows = video.shape[2]
    cols = video.shape[3]
    chans = video.shape[4]
    past = passed_along(lax.slice_in_dim(video, frames - 2, None, axis=1), "group", 1)
    vwide = row_halo(jnp.concatenate([past, video], axis=1), "space", 2)
    pos_wide, same_fwd, same_bwd = clip_tables(clip_id, frames)
    omega = 0.37 * (jnp.arange(chans) % 8 + 1).astype(jnp.float32)
    embed = jnp.sin(pos_wide.astype(jnp.float32)[:, :, None] * omega)
    shifted = (vwide.astype(jnp.float32) + embed[:, :, None, None, :]).astype(jnp.bfloat16)
    row = jnp.arange(rows + 2)
    where_s = lax.axis_index("space")
    inside = ((row > 0) | (where_s > 0)) & ((row < rows + 1) | (where_s < lax.axis_size("space") - 1))
    shifted = jnp.where(inside[None, None, :, None, None], shifted, jnp.zeros_like(shifted))
    maskf = same_fwd.astype(jnp.float32)
    widened = jnp.pad(shifted, ((0, 0), (0, 0), (0, 0), (1, 1), (0, 0)))
    stacked = jnp.concatenate([widened[:, :, :, b : b + cols] for b in range(3)], axis=4)
    taps = weight.reshape(3, 3, 3 * chans, chans)
    pre = jnp.zeros(video.shape, jnp.float32)
    for k in range(3):
        part = jnp.zeros(video.shape, jnp.float32)
        for a in range(3):
            block = stacked[:, 2 - k : 2 - k + frames, a : a + rows]
            part = part + jnp.einsum(
                "sfhwk,kc->sfhwc", block, taps[k, a], preferred_element_type=jnp.float32
            )
        pre = pre + part * maskf[k][:, :, None, None, None]
    sigma = jax.nn.sigmoid(pre)
    activation = (pre * sigma).astype(jnp.bfloat16)
    delta = (cotangent.astype(jnp.float32) * sigma * (1.0 + pre * (1.0 - sigma))).astype(
        jnp.bfloat16
    )
    ahead = passed_along(lax.slice_in_dim(delta, 0, 2, axis=1), "group", -1)
    gwide = row_halo(jnp.concatenate([delta, ahead], axis=1), "space", 2)
    terms = []
    for k in range(3):
        masked = delta * same_fwd[k].astype(jnp.bfloat16)[:, :, None, None, None]
        for a in range(3):
            block = stacked[:, 2 - k : 2 - k + frames, a : a + rows]
            block = block.reshape(block.shape[:4] + (3, chans))
            terms.append(
                jnp.einsum("sfhwbi,sfhwc->ibc", block, masked, preferred_element_type=jnp.float32)
            )
    total = jnp.stack(terms, axis=1).reshape(chans, 27, chans)
    ng, nd, ns = lax.axis_size("group"), lax.axis_size("dp"), lax.axis_size("space")
    total = total.reshape(ng * nd, ns, 27, chans)
    if STAGED:
        where = lax.axis_index("space")
        keep = lax.dynamic_index_in_dim(total, where, axis=1, keepdims=False)
        give = lax.dynamic_index_in_dim(total, 1 - where, axis=1, keepdims=False)
        total = keep + lax.ppermute(give, "space", [(0, 1), (1, 0)])
    else:
        total = lax.psum_scatter(total, "space", scatter_dimension=1, tiled=True)
        total = total.reshape(ng * nd, 27, chans)
    total = lax.psum_scatter(total, ("group", "dp"), scatter_dimension=0, tiled=True)
    reduced = total.reshape(27, chans)
    gwide = jnp.pad(gwide, ((0, 0), (0, 0), (0, 0), (1, 1), (0, 0)))
    gstack = jnp.concatenate([gwide[:, :, :, 2 - b : 2 - b + cols] for b in range(3)], axis=4)
    back = (
        weight.reshape(3, 3, 3, chans, chans)
        .transpose(0, 1, 2, 4, 3)
        .reshape(3, 3, 3 * chans, chans)
    )
    grad = jnp.zeros(video.shape, jnp.float32)
    for k in range(3):
        part = jnp.zeros(video.shape, jnp.float32)
        for a in range(3):
            block = gstack[:, k : k + frames, 2 - a : 2 - a + rows]
            part = part + jnp.einsum(
                "sfhwk,kc->sfhwc", block, back[k, a], preferred_element_type=jnp.float32
            )
        grad = grad + part * same_bwd[k].astype(jnp.float32)[:, :, None, None, None]
    return (activation, grad.astype(jnp.bfloat16), reduced)


def solution(mesh):
    placed = (
        P("dp", "group", "space", None, None),
        P("dp", "group", "space", None, None),
        P(),
        P("dp", "group"),
    )
    return jax.shard_map(
        local,
        mesh=mesh,
        in_specs=placed,
        out_specs=(
            P("dp", "group", "space", None, None),
            P("dp", "group", "space", None, None),
            P(None, ("group", "dp", "space")),
        ),
        check_vma=False,
    )
```

```python
import jax
import jax.numpy as jnp
from jax import lax
from jax.sharding import PartitionSpec as P


def passed_along(value, axis, by):
    length = lax.axis_size(axis)
    pairs = [(i, i + by) for i in range(length) if 0 <= i + by < length]
    return lax.ppermute(value, axis, pairs)


def row_halo(block, axis, dim):
    count = lax.axis_size(axis)
    forward = [(i, i + 1) for i in range(count - 1)]
    backward = [(target, source) for source, target in forward]
    low = lax.ppermute(
        lax.slice_in_dim(block, block.shape[dim] - 1, None, axis=dim), axis, forward
    )
    high = lax.ppermute(lax.slice_in_dim(block, 0, 1, axis=dim), axis, backward)
    return jnp.concatenate([low, block, high], axis=dim)


def ring_pairs(axis, shift, sub):
    count = lax.axis_size(axis)
    inner, outer = sub
    pairs = []
    for i in range(count):
        hi, mid, lo = i // (inner * outer), (i // inner) % outer, i % inner
        pairs.append((i, (hi * outer + (mid + shift) % outer) * inner + lo))
    return pairs


def ring_scatter(x, ring, dim):
    axis, sub = ring
    inner, outer = sub
    n = outer
    pos = (lax.axis_index(axis) // inner) % outer
    half = x.shape[-1] // 2
    xa, xb = x[..., :half], x[..., half:]

    def take(arr, idx):
        return lax.dynamic_slice_in_dim(arr, idx % n, 1, axis=dim)

    acc_a = take(xa, pos - 1)
    acc_b = take(xb, pos + 1)
    for j in range(n - 1):
        recv_a = lax.ppermute(acc_a, axis, ring_pairs(axis, 1, sub))
        recv_b = lax.ppermute(acc_b, axis, ring_pairs(axis, -1, sub))
        acc_a = recv_a + take(xa, pos - j - 2)
        acc_b = recv_b + take(xb, pos + j + 2)
    return jnp.concatenate([acc_a, acc_b], axis=-1)


def reduce_weight_grad(total):
    chans, ntaps, outs = total.shape
    ng, nd, ns = lax.axis_size("group"), lax.axis_size("dp"), lax.axis_size("space")
    across = 4 if ng % 4 == 0 else ng
    down = ng // across
    total = total.reshape(down, across, nd, ns, ntaps, outs)
    where = lax.axis_index("space")
    keep = lax.dynamic_index_in_dim(total, where, axis=3, keepdims=False)
    give = lax.dynamic_index_in_dim(total, ns - 1 - where, axis=3, keepdims=False)
    total = keep + lax.ppermute(give, "space", [(0, 1), (1, 0)])
    rings = {
        0: ("group", (across, down)),
        1: ("group", (1, across)),
        2: ("dp", (1, nd)),
    }
    orders = ((2, 1, 0), (1, 0, 2), (0, 2, 1))
    per = ntaps // len(orders)
    parts = []
    for n, order in enumerate(orders):
        part = total[:, :, :, n * per : (n + 1) * per]
        for dim in order:
            part = ring_scatter(part, rings[dim], dim)
        parts.append(part.reshape(per, outs))
    return jnp.concatenate(parts, axis=0)


def clip_tables(clip_id, frames):
    ids = lax.all_gather(clip_id, "group", axis=1, tiled=True)
    total = ids.shape[1]
    index = jnp.arange(total, dtype=jnp.int32)[None, :]
    prev = jnp.concatenate([jnp.full_like(ids[:, :1], -1), ids[:, :-1]], axis=1)
    boundary = ids != prev
    start = lax.cummax(jnp.where(boundary, index, 0), axis=1)
    position = index - start
    ext = jnp.concatenate([jnp.full_like(ids[:, :2], -1), ids], axis=1)
    same = jnp.stack([ext[:, 2 - k : 2 - k + total] == ids for k in range(3)], axis=0)
    first = lax.axis_index("group") * frames
    pos_pad = jnp.concatenate([jnp.zeros_like(position[:, :2]), position], axis=1)
    pos_wide = lax.dynamic_slice_in_dim(pos_pad, first, frames + 2, axis=1)
    same_pad = jnp.concatenate([same, jnp.zeros_like(same[:, :, :2])], axis=2)
    own = lax.dynamic_slice_in_dim(same_pad, first, frames + 2, axis=2)
    fwd = own[:, :, :frames]
    bwd = jnp.stack([own[k, :, k : k + frames] for k in range(3)], axis=0)
    return pos_wide, fwd, bwd


def local(video, cotangent, weight, clip_id):
    frames = video.shape[1]
    rows = video.shape[2]
    cols = video.shape[3]
    chans = video.shape[4]
    past = passed_along(lax.slice_in_dim(video, frames - 2, None, axis=1), "group", 1)
    vwide = row_halo(jnp.concatenate([past, video], axis=1), "space", 2)
    pos_wide, same_fwd, same_bwd = clip_tables(clip_id, frames)
    omega = 0.37 * (jnp.arange(chans) % 8 + 1).astype(jnp.float32)
    embed = jnp.sin(pos_wide.astype(jnp.float32)[:, :, None] * omega)
    shifted = (vwide.astype(jnp.float32) + embed[:, :, None, None, :]).astype(jnp.bfloat16)
    row = jnp.arange(rows + 2)
    where_s = lax.axis_index("space")
    inside = ((row > 0) | (where_s > 0)) & ((row < rows + 1) | (where_s < lax.axis_size("space") - 1))
    shifted = jnp.where(inside[None, None, :, None, None], shifted, jnp.zeros_like(shifted))
    maskf = same_fwd.astype(jnp.float32)
    widened = jnp.pad(shifted, ((0, 0), (0, 0), (0, 0), (1, 1), (0, 0)))
    stacked = jnp.concatenate([widened[:, :, :, b : b + cols] for b in range(3)], axis=4)
    taps = weight.reshape(3, 3, 3 * chans, chans)
    pre = jnp.zeros(video.shape, jnp.float32)
    for k in range(3):
        part = jnp.zeros(video.shape, jnp.float32)
        for a in range(3):
            block = stacked[:, 2 - k : 2 - k + frames, a : a + rows]
            part = part + jnp.einsum(
                "sfhwk,kc->sfhwc", block, taps[k, a], preferred_element_type=jnp.float32
            )
        pre = pre + part * maskf[k][:, :, None, None, None]
    sigma = jax.nn.sigmoid(pre)
    activation = (pre * sigma).astype(jnp.bfloat16)
    delta = (cotangent.astype(jnp.float32) * sigma * (1.0 + pre * (1.0 - sigma))).astype(
        jnp.bfloat16
    )
    ahead = passed_along(lax.slice_in_dim(delta, 0, 2, axis=1), "group", -1)
    gwide = row_halo(jnp.concatenate([delta, ahead], axis=1), "space", 2)
    terms = []
    for k in range(3):
        masked = delta * same_fwd[k].astype(jnp.bfloat16)[:, :, None, None, None]
        for a in range(3):
            block = stacked[:, 2 - k : 2 - k + frames, a : a + rows]
            block = block.reshape(block.shape[:4] + (3, chans))
            terms.append(
                jnp.einsum("sfhwbi,sfhwc->ibc", block, masked, preferred_element_type=jnp.float32)
            )
    total = jnp.stack(terms, axis=1).reshape(chans, 27, chans)
    reduced = reduce_weight_grad(total.reshape(chans, 27, chans))
    gwide = jnp.pad(gwide, ((0, 0), (0, 0), (0, 0), (1, 1), (0, 0)))
    gstack = jnp.concatenate([gwide[:, :, :, 2 - b : 2 - b + cols] for b in range(3)], axis=4)
    back = (
        weight.reshape(3, 3, 3, chans, chans)
        .transpose(0, 1, 2, 4, 3)
        .reshape(3, 3, 3 * chans, chans)
    )
    grad = jnp.zeros(video.shape, jnp.float32)
    for k in range(3):
        part = jnp.zeros(video.shape, jnp.float32)
        for a in range(3):
            block = gstack[:, k : k + frames, 2 - a : 2 - a + rows]
            part = part + jnp.einsum(
                "sfhwk,kc->sfhwc", block, back[k, a], preferred_element_type=jnp.float32
            )
        grad = grad + part * same_bwd[k].astype(jnp.float32)[:, :, None, None, None]
    return (activation, grad.astype(jnp.bfloat16), reduced)


def solution(mesh):
    placed = (
        P("dp", "group", "space", None, None),
        P("dp", "group", "space", None, None),
        P(),
        P("dp", "group"),
    )
    return jax.shard_map(
        local,
        mesh=mesh,
        in_specs=placed,
        out_specs=(
            P("dp", "group", "space", None, None),
            P("dp", "group", "space", None, None),
            P(None, ("group", "dp", "space")),
        ),
        check_vma=False,
    )
```

```python
import jax
import jax.numpy as jnp
from jax import lax
from jax.sharding import PartitionSpec as P


def passed_along(value, axis, by):
    length = lax.axis_size(axis)
    pairs = [(i, i + by) for i in range(length) if 0 <= i + by < length]
    return lax.ppermute(value, axis, pairs)


def row_halo(block, axis, dim):
    count = lax.axis_size(axis)
    forward = [(i, i + 1) for i in range(count - 1)]
    backward = [(target, source) for source, target in forward]
    low = lax.ppermute(
        lax.slice_in_dim(block, block.shape[dim] - 1, None, axis=dim), axis, forward
    )
    high = lax.ppermute(lax.slice_in_dim(block, 0, 1, axis=dim), axis, backward)
    return jnp.concatenate([low, block, high], axis=dim)


def halve(x, dim, axis, flip):
    bit = (lax.axis_index(axis) // flip) % 2
    keep = lax.dynamic_slice_in_dim(x, bit, 1, axis=dim)
    give = lax.dynamic_slice_in_dim(x, 1 - bit, 1, axis=dim)
    pairs = [(i, i ^ flip) for i in range(lax.axis_size(axis))]
    return keep + lax.ppermute(give, axis, pairs)


def bits_of(n):
    count = n.bit_length() - 1
    assert 1 << count == n
    return count


def reduce_weight_grad(total):
    chans, ntaps, outs = total.shape
    ng, nd, ns = lax.axis_size("group"), lax.axis_size("dp"), lax.axis_size("space")
    across = 4 if ng % 4 == 0 else ng
    down = ng // across
    digits = []
    for name, axis, size, step in (
        ("y", "group", down, across),
        ("x", "group", across, 1),
        ("d", "dp", nd, 1),
        ("s", "space", ns, 1),
    ):
        digits += [(name, b, axis, step << b) for b in reversed(range(bits_of(size)))]
    total = total.reshape((2,) * len(digits) + (ntaps, outs))
    place = {(name, b): n for n, (name, b, _, _) in enumerate(digits)}
    info = {(name, b): (axis, flip) for name, b, axis, flip in digits}

    def step(x, key):
        axis, flip = info[key]
        return halve(x, place[key], axis, flip)

    total = step(total, ("s", 0))
    ys = [("y", b) for b in range(bits_of(down))]
    xs = [("x", b) for b in range(bits_of(across))]
    ds = [("d", b) for b in range(bits_of(nd))]
    lanes = (ds, xs, ys)
    parts = []
    per = ntaps // 3
    for n in range(3):
        rotated = lanes[n:] + lanes[:n]
        order = []
        for level in range(max(len(lane) for lane in lanes)):
            order += [lane[level] for lane in rotated if level < len(lane)]
        part = total[..., n * per : (n + 1) * per, :]
        for key in order:
            part = step(part, key)
        parts.append(part.reshape(per, outs))
    return jnp.concatenate(parts, axis=0)


def clip_tables(clip_id, frames):
    ids = lax.all_gather(clip_id, "group", axis=1, tiled=True)
    total = ids.shape[1]
    index = jnp.arange(total, dtype=jnp.int32)[None, :]
    prev = jnp.concatenate([jnp.full_like(ids[:, :1], -1), ids[:, :-1]], axis=1)
    boundary = ids != prev
    start = lax.cummax(jnp.where(boundary, index, 0), axis=1)
    position = index - start
    ext = jnp.concatenate([jnp.full_like(ids[:, :2], -1), ids], axis=1)
    same = jnp.stack([ext[:, 2 - k : 2 - k + total] == ids for k in range(3)], axis=0)
    first = lax.axis_index("group") * frames
    pos_pad = jnp.concatenate([jnp.zeros_like(position[:, :2]), position], axis=1)
    pos_wide = lax.dynamic_slice_in_dim(pos_pad, first, frames + 2, axis=1)
    same_pad = jnp.concatenate([same, jnp.zeros_like(same[:, :, :2])], axis=2)
    own = lax.dynamic_slice_in_dim(same_pad, first, frames + 2, axis=2)
    fwd = own[:, :, :frames]
    bwd = jnp.stack([own[k, :, k : k + frames] for k in range(3)], axis=0)
    return pos_wide, fwd, bwd


def local(video, cotangent, weight, clip_id):
    frames = video.shape[1]
    rows = video.shape[2]
    cols = video.shape[3]
    chans = video.shape[4]
    past = passed_along(lax.slice_in_dim(video, frames - 2, None, axis=1), "group", 1)
    vwide = row_halo(jnp.concatenate([past, video], axis=1), "space", 2)
    pos_wide, same_fwd, same_bwd = clip_tables(clip_id, frames)
    omega = 0.37 * (jnp.arange(chans) % 8 + 1).astype(jnp.float32)
    embed = jnp.sin(pos_wide.astype(jnp.float32)[:, :, None] * omega)
    shifted = (vwide.astype(jnp.float32) + embed[:, :, None, None, :]).astype(jnp.bfloat16)
    row = jnp.arange(rows + 2)
    where_s = lax.axis_index("space")
    inside = ((row > 0) | (where_s > 0)) & ((row < rows + 1) | (where_s < lax.axis_size("space") - 1))
    shifted = jnp.where(inside[None, None, :, None, None], shifted, jnp.zeros_like(shifted))
    maskf = same_fwd.astype(jnp.float32)
    widened = jnp.pad(shifted, ((0, 0), (0, 0), (0, 0), (1, 1), (0, 0)))
    stacked = jnp.concatenate([widened[:, :, :, b : b + cols] for b in range(3)], axis=4)
    taps = weight.reshape(3, 3, 3 * chans, chans)
    pre = jnp.zeros(video.shape, jnp.float32)
    for k in range(3):
        part = jnp.zeros(video.shape, jnp.float32)
        for a in range(3):
            block = stacked[:, 2 - k : 2 - k + frames, a : a + rows]
            part = part + jnp.einsum(
                "sfhwk,kc->sfhwc", block, taps[k, a], preferred_element_type=jnp.float32
            )
        pre = pre + part * maskf[k][:, :, None, None, None]
    sigma = jax.nn.sigmoid(pre)
    activation = (pre * sigma).astype(jnp.bfloat16)
    delta = (cotangent.astype(jnp.float32) * sigma * (1.0 + pre * (1.0 - sigma))).astype(
        jnp.bfloat16
    )
    ahead = passed_along(lax.slice_in_dim(delta, 0, 2, axis=1), "group", -1)
    gwide = row_halo(jnp.concatenate([delta, ahead], axis=1), "space", 2)
    terms = []
    for k in range(3):
        masked = delta * same_fwd[k].astype(jnp.bfloat16)[:, :, None, None, None]
        for a in range(3):
            block = stacked[:, 2 - k : 2 - k + frames, a : a + rows]
            block = block.reshape(block.shape[:4] + (3, chans))
            terms.append(
                jnp.einsum("sfhwbi,sfhwc->ibc", block, masked, preferred_element_type=jnp.float32)
            )
    total = jnp.stack(terms, axis=1).reshape(chans, 27, chans)
    reduced = reduce_weight_grad(total.reshape(chans, 27, chans))
    gwide = jnp.pad(gwide, ((0, 0), (0, 0), (0, 0), (1, 1), (0, 0)))
    gstack = jnp.concatenate([gwide[:, :, :, 2 - b : 2 - b + cols] for b in range(3)], axis=4)
    back = (
        weight.reshape(3, 3, 3, chans, chans)
        .transpose(0, 1, 2, 4, 3)
        .reshape(3, 3, 3 * chans, chans)
    )
    grad = jnp.zeros(video.shape, jnp.float32)
    for k in range(3):
        part = jnp.zeros(video.shape, jnp.float32)
        for a in range(3):
            block = gstack[:, k : k + frames, 2 - a : 2 - a + rows]
            part = part + jnp.einsum(
                "sfhwk,kc->sfhwc", block, back[k, a], preferred_element_type=jnp.float32
            )
        grad = grad + part * same_bwd[k].astype(jnp.float32)[:, :, None, None, None]
    return (activation, grad.astype(jnp.bfloat16), reduced)


def solution(mesh):
    placed = (
        P("dp", "group", "space", None, None),
        P("dp", "group", "space", None, None),
        P(),
        P("dp", "group"),
    )
    return jax.shard_map(
        local,
        mesh=mesh,
        in_specs=placed,
        out_specs=(
            P("dp", "group", "space", None, None),
            P("dp", "group", "space", None, None),
            P(None, ("group", "dp", "space")),
        ),
        check_vma=False,
    )
```

```python
import jax
import jax.numpy as jnp
from jax import lax
from jax.sharding import PartitionSpec as P


def passed_along(value, axis, by):
    length = lax.axis_size(axis)
    pairs = [(i, i + by) for i in range(length) if 0 <= i + by < length]
    return lax.ppermute(value, axis, pairs)


def row_halo(block, axis, dim):
    count = lax.axis_size(axis)
    forward = [(i, i + 1) for i in range(count - 1)]
    backward = [(target, source) for source, target in forward]
    low = lax.ppermute(
        lax.slice_in_dim(block, block.shape[dim] - 1, None, axis=dim), axis, forward
    )
    high = lax.ppermute(lax.slice_in_dim(block, 0, 1, axis=dim), axis, backward)
    return jnp.concatenate([low, block, high], axis=dim)


def halve(x, dim, axis, flip):
    size = x.shape[dim] // 2
    bit = (lax.axis_index(axis) // flip) % 2
    keep = lax.dynamic_slice_in_dim(x, bit * size, size, axis=dim)
    give = lax.dynamic_slice_in_dim(x, (1 - bit) * size, size, axis=dim)
    pairs = [(i, i ^ flip) for i in range(lax.axis_size(axis))]
    return keep + lax.ppermute(give, axis, pairs)


def bits_of(n):
    count = n.bit_length() - 1
    assert 1 << count == n
    return count


def owner_pairs(order, sizes):
    names = ("group", "dp", "space")
    count = sizes["group"] * sizes["dp"] * sizes["space"]
    pairs = []
    for linear in range(count):
        where = {
            "group": linear // (sizes["dp"] * sizes["space"]),
            "dp": (linear // sizes["space"]) % sizes["dp"],
            "space": linear % sizes["space"],
        }
        chunk = 0
        for axis, flip in order:
            chunk = chunk * 2 + (where[axis] // flip) % 2
        pairs.append((linear, chunk))
    return names, pairs


def reduce_weight_grad(total):
    ntaps, chans, outs = total.shape
    sizes = {name: lax.axis_size(name) for name in ("group", "dp", "space")}
    ng = sizes["group"]
    across = 4 if ng % 4 == 0 else ng
    down = ng // across
    assert chans == ng * sizes["dp"] * sizes["space"]
    first = ("space", 1)
    ys = [("group", across << b) for b in range(bits_of(down))]
    xs = [("group", 1 << b) for b in range(bits_of(across))]
    ds = [("dp", 1 << b) for b in range(bits_of(sizes["dp"]))]
    assert sizes["space"] == 2
    lanes = (ds, xs, ys)
    total = halve(total, 1, *first)
    parts = []
    per = ntaps // 3
    for n in range(3):
        rotated = lanes[n:] + lanes[:n]
        order = [first]
        for level in range(max(len(lane) for lane in lanes)):
            order += [lane[level] for lane in rotated if level < len(lane)]
        part = total[n * per : (n + 1) * per]
        for axis, flip in order[1:]:
            part = halve(part, 1, axis, flip)
        names, pairs = owner_pairs(order, sizes)
        part = lax.ppermute(part, names, pairs)
        parts.append(part.reshape(per, outs))
    return jnp.concatenate(parts, axis=0)


def clip_tables(clip_id, frames):
    ids = lax.all_gather(clip_id, "group", axis=1, tiled=True)
    total = ids.shape[1]
    index = jnp.arange(total, dtype=jnp.int32)[None, :]
    prev = jnp.concatenate([jnp.full_like(ids[:, :1], -1), ids[:, :-1]], axis=1)
    boundary = ids != prev
    start = lax.cummax(jnp.where(boundary, index, 0), axis=1)
    position = index - start
    ext = jnp.concatenate([jnp.full_like(ids[:, :2], -1), ids], axis=1)
    same = jnp.stack([ext[:, 2 - k : 2 - k + total] == ids for k in range(3)], axis=0)
    first = lax.axis_index("group") * frames
    pos_pad = jnp.concatenate([jnp.zeros_like(position[:, :2]), position], axis=1)
    pos_wide = lax.dynamic_slice_in_dim(pos_pad, first, frames + 2, axis=1)
    same_pad = jnp.concatenate([same, jnp.zeros_like(same[:, :, :2])], axis=2)
    own = lax.dynamic_slice_in_dim(same_pad, first, frames + 2, axis=2)
    fwd = own[:, :, :frames]
    bwd = jnp.stack([own[k, :, k : k + frames] for k in range(3)], axis=0)
    return pos_wide, fwd, bwd


def local(video, cotangent, weight, clip_id):
    frames = video.shape[1]
    rows = video.shape[2]
    cols = video.shape[3]
    chans = video.shape[4]
    past = passed_along(lax.slice_in_dim(video, frames - 2, None, axis=1), "group", 1)
    vwide = row_halo(jnp.concatenate([past, video], axis=1), "space", 2)
    pos_wide, same_fwd, same_bwd = clip_tables(clip_id, frames)
    omega = 0.37 * (jnp.arange(chans) % 8 + 1).astype(jnp.float32)
    embed = jnp.sin(pos_wide.astype(jnp.float32)[:, :, None] * omega)
    shifted = (vwide.astype(jnp.float32) + embed[:, :, None, None, :]).astype(jnp.bfloat16)
    row = jnp.arange(rows + 2)
    where_s = lax.axis_index("space")
    inside = ((row > 0) | (where_s > 0)) & ((row < rows + 1) | (where_s < lax.axis_size("space") - 1))
    shifted = jnp.where(inside[None, None, :, None, None], shifted, jnp.zeros_like(shifted))
    maskf = same_fwd.astype(jnp.float32)
    widened = jnp.pad(shifted, ((0, 0), (0, 0), (0, 0), (1, 1), (0, 0)))
    stacked = jnp.concatenate([widened[:, :, :, b : b + cols] for b in range(3)], axis=4)
    taps = weight.reshape(3, 3, 3 * chans, chans)
    pre = jnp.zeros(video.shape, jnp.float32)
    for k in range(3):
        part = jnp.zeros(video.shape, jnp.float32)
        for a in range(3):
            block = stacked[:, 2 - k : 2 - k + frames, a : a + rows]
            part = part + jnp.einsum(
                "sfhwk,kc->sfhwc", block, taps[k, a], preferred_element_type=jnp.float32
            )
        pre = pre + part * maskf[k][:, :, None, None, None]
    sigma = jax.nn.sigmoid(pre)
    activation = (pre * sigma).astype(jnp.bfloat16)
    delta = (cotangent.astype(jnp.float32) * sigma * (1.0 + pre * (1.0 - sigma))).astype(
        jnp.bfloat16
    )
    ahead = passed_along(lax.slice_in_dim(delta, 0, 2, axis=1), "group", -1)
    gwide = row_halo(jnp.concatenate([delta, ahead], axis=1), "space", 2)
    terms = []
    for k in range(3):
        masked = delta * same_fwd[k].astype(jnp.bfloat16)[:, :, None, None, None]
        for a in range(3):
            block = stacked[:, 2 - k : 2 - k + frames, a : a + rows]
            terms.append(
                jnp.einsum("sfhwk,sfhwc->kc", block, masked, preferred_element_type=jnp.float32)
            )
    total = jnp.stack(terms).reshape(27, chans, chans)
    reduced = reduce_weight_grad(total)
    gwide = jnp.pad(gwide, ((0, 0), (0, 0), (0, 0), (1, 1), (0, 0)))
    gstack = jnp.concatenate([gwide[:, :, :, 2 - b : 2 - b + cols] for b in range(3)], axis=4)
    back = (
        weight.reshape(3, 3, 3, chans, chans)
        .transpose(0, 1, 2, 4, 3)
        .reshape(3, 3, 3 * chans, chans)
    )
    grad = jnp.zeros(video.shape, jnp.float32)
    for k in range(3):
        part = jnp.zeros(video.shape, jnp.float32)
        for a in range(3):
            block = gstack[:, k : k + frames, 2 - a : 2 - a + rows]
            part = part + jnp.einsum(
                "sfhwk,kc->sfhwc", block, back[k, a], preferred_element_type=jnp.float32
            )
        grad = grad + part * same_bwd[k].astype(jnp.float32)[:, :, None, None, None]
    return (activation, grad.astype(jnp.bfloat16), reduced)


def solution(mesh):
    placed = (
        P("dp", "group", "space", None, None),
        P("dp", "group", "space", None, None),
        P(),
        P("dp", "group"),
    )
    return jax.shard_map(
        local,
        mesh=mesh,
        in_specs=placed,
        out_specs=(
            P("dp", "group", "space", None, None),
            P("dp", "group", "space", None, None),
            P(None, ("group", "dp", "space")),
        ),
        check_vma=False,
    )
```

```python
import jax
import jax.numpy as jnp
from jax import lax
from jax.sharding import PartitionSpec as P


def passed_along(value, axis, by):
    length = lax.axis_size(axis)
    pairs = [(i, i + by) for i in range(length) if 0 <= i + by < length]
    return lax.ppermute(value, axis, pairs)


def row_halo(block, axis, dim):
    count = lax.axis_size(axis)
    forward = [(i, i + 1) for i in range(count - 1)]
    backward = [(target, source) for source, target in forward]
    low = lax.ppermute(
        lax.slice_in_dim(block, block.shape[dim] - 1, None, axis=dim), axis, forward
    )
    high = lax.ppermute(lax.slice_in_dim(block, 0, 1, axis=dim), axis, backward)
    return jnp.concatenate([low, block, high], axis=dim)


def halve(x, dim, axis, flip):
    size = x.shape[dim] // 2
    bit = (lax.axis_index(axis) // flip) % 2
    keep = lax.dynamic_slice_in_dim(x, bit * size, size, axis=dim)
    give = lax.dynamic_slice_in_dim(x, (1 - bit) * size, size, axis=dim)
    pairs = [(i, i ^ flip) for i in range(lax.axis_size(axis))]
    return keep + lax.ppermute(give, axis, pairs)


def bits_of(n):
    count = n.bit_length() - 1
    assert 1 << count == n
    return count


def owner_pairs(order, sizes):
    names = ("group", "dp", "space")
    count = sizes["group"] * sizes["dp"] * sizes["space"]
    pairs = []
    for linear in range(count):
        where = {
            "group": linear // (sizes["dp"] * sizes["space"]),
            "dp": (linear // sizes["space"]) % sizes["dp"],
            "space": linear % sizes["space"],
        }
        chunk = 0
        for axis, flip in order:
            chunk = chunk * 2 + (where[axis] // flip) % 2
        pairs.append((linear, chunk))
    return names, pairs


def reduce_weight_grad(total):
    ntaps, chans, outs = total.shape
    sizes = {name: lax.axis_size(name) for name in ("group", "dp", "space")}
    ng = sizes["group"]
    across = 4 if ng % 4 == 0 else ng
    down = ng // across
    assert chans == ng * sizes["dp"] * sizes["space"]
    first = ("space", 1)
    ys = [("group", across << b) for b in range(bits_of(down))]
    xs = [("group", 1 << b) for b in range(bits_of(across))]
    ds = [("dp", 1 << b) for b in range(bits_of(sizes["dp"]))]
    assert sizes["space"] == 2
    lanes = (ds, xs, ys)
    total = halve(total, 1, *first)
    spread = [lane[0] for lane in lanes]
    rest = [key for lane in (xs, ys, ds) for key in lane[1:]]
    per = ntaps // len(lanes)
    parts, orders = [], []
    for n in range(len(lanes)):
        order = [first] + spread[n:] + spread[:n]
        part = total[n * per : (n + 1) * per]
        for axis, flip in order[1:]:
            part = halve(part, 1, axis, flip)
        parts.append(part)
        orders.append(order + rest)
    joined = jnp.stack(parts)
    for axis, flip in rest:
        joined = halve(joined, 2, axis, flip)
    parts = []
    for n, order in enumerate(orders):
        names, pairs = owner_pairs(order, sizes)
        parts.append(lax.ppermute(joined[n], names, pairs).reshape(per, outs))
    return jnp.concatenate(parts, axis=0)


def clip_tables(clip_id, frames):
    ids = lax.all_gather(clip_id, "group", axis=1, tiled=True)
    total = ids.shape[1]
    index = jnp.arange(total, dtype=jnp.int32)[None, :]
    prev = jnp.concatenate([jnp.full_like(ids[:, :1], -1), ids[:, :-1]], axis=1)
    boundary = ids != prev
    start = lax.cummax(jnp.where(boundary, index, 0), axis=1)
    position = index - start
    ext = jnp.concatenate([jnp.full_like(ids[:, :2], -1), ids], axis=1)
    same = jnp.stack([ext[:, 2 - k : 2 - k + total] == ids for k in range(3)], axis=0)
    first = lax.axis_index("group") * frames
    pos_pad = jnp.concatenate([jnp.zeros_like(position[:, :2]), position], axis=1)
    pos_wide = lax.dynamic_slice_in_dim(pos_pad, first, frames + 2, axis=1)
    same_pad = jnp.concatenate([same, jnp.zeros_like(same[:, :, :2])], axis=2)
    own = lax.dynamic_slice_in_dim(same_pad, first, frames + 2, axis=2)
    fwd = own[:, :, :frames]
    bwd = jnp.stack([own[k, :, k : k + frames] for k in range(3)], axis=0)
    return pos_wide, fwd, bwd


def local(video, cotangent, weight, clip_id):
    frames = video.shape[1]
    rows = video.shape[2]
    cols = video.shape[3]
    chans = video.shape[4]
    past = passed_along(lax.slice_in_dim(video, frames - 2, None, axis=1), "group", 1)
    vwide = row_halo(jnp.concatenate([past, video], axis=1), "space", 2)
    pos_wide, same_fwd, same_bwd = clip_tables(clip_id, frames)
    omega = 0.37 * (jnp.arange(chans) % 8 + 1).astype(jnp.float32)
    embed = jnp.sin(pos_wide.astype(jnp.float32)[:, :, None] * omega)
    shifted = (vwide.astype(jnp.float32) + embed[:, :, None, None, :]).astype(jnp.bfloat16)
    row = jnp.arange(rows + 2)
    where_s = lax.axis_index("space")
    inside = ((row > 0) | (where_s > 0)) & ((row < rows + 1) | (where_s < lax.axis_size("space") - 1))
    shifted = jnp.where(inside[None, None, :, None, None], shifted, jnp.zeros_like(shifted))
    maskf = same_fwd.astype(jnp.float32)
    widened = jnp.pad(shifted, ((0, 0), (0, 0), (0, 0), (1, 1), (0, 0)))
    stacked = jnp.concatenate([widened[:, :, :, b : b + cols] for b in range(3)], axis=4)
    taps = weight.reshape(3, 3, 3 * chans, chans)
    pre = jnp.zeros(video.shape, jnp.float32)
    for k in range(3):
        part = jnp.zeros(video.shape, jnp.float32)
        for a in range(3):
            block = stacked[:, 2 - k : 2 - k + frames, a : a + rows]
            part = part + jnp.einsum(
                "sfhwk,kc->sfhwc", block, taps[k, a], preferred_element_type=jnp.float32
            )
        pre = pre + part * maskf[k][:, :, None, None, None]
    sigma = jax.nn.sigmoid(pre)
    activation = (pre * sigma).astype(jnp.bfloat16)
    delta = (cotangent.astype(jnp.float32) * sigma * (1.0 + pre * (1.0 - sigma))).astype(
        jnp.bfloat16
    )
    ahead = passed_along(lax.slice_in_dim(delta, 0, 2, axis=1), "group", -1)
    gwide = row_halo(jnp.concatenate([delta, ahead], axis=1), "space", 2)
    terms = []
    for k in range(3):
        masked = delta * same_fwd[k].astype(jnp.bfloat16)[:, :, None, None, None]
        for a in range(3):
            block = stacked[:, 2 - k : 2 - k + frames, a : a + rows]
            terms.append(
                jnp.einsum("sfhwk,sfhwc->kc", block, masked, preferred_element_type=jnp.float32)
            )
    total = jnp.stack(terms).reshape(27, chans, chans)
    reduced = reduce_weight_grad(total)
    gwide = jnp.pad(gwide, ((0, 0), (0, 0), (0, 0), (1, 1), (0, 0)))
    gstack = jnp.concatenate([gwide[:, :, :, 2 - b : 2 - b + cols] for b in range(3)], axis=4)
    back = (
        weight.reshape(3, 3, 3, chans, chans)
        .transpose(0, 1, 2, 4, 3)
        .reshape(3, 3, 3 * chans, chans)
    )
    grad = jnp.zeros(video.shape, jnp.float32)
    for k in range(3):
        part = jnp.zeros(video.shape, jnp.float32)
        for a in range(3):
            block = gstack[:, k : k + frames, 2 - a : 2 - a + rows]
            part = part + jnp.einsum(
                "sfhwk,kc->sfhwc", block, back[k, a], preferred_element_type=jnp.float32
            )
        grad = grad + part * same_bwd[k].astype(jnp.float32)[:, :, None, None, None]
    return (activation, grad.astype(jnp.bfloat16), reduced)


def solution(mesh):
    placed = (
        P("dp", "group", "space", None, None),
        P("dp", "group", "space", None, None),
        P(),
        P("dp", "group"),
    )
    return jax.shard_map(
        local,
        mesh=mesh,
        in_specs=placed,
        out_specs=(
            P("dp", "group", "space", None, None),
            P("dp", "group", "space", None, None),
            P(None, ("group", "dp", "space")),
        ),
        check_vma=False,
    )
```

```python
import jax
import jax.numpy as jnp
from jax import lax
from jax.sharding import PartitionSpec as P


def passed_along(value, axis, by):
    length = lax.axis_size(axis)
    pairs = [(i, i + by) for i in range(length) if 0 <= i + by < length]
    return lax.ppermute(value, axis, pairs)


def row_halo(block, axis, dim):
    count = lax.axis_size(axis)
    forward = [(i, i + 1) for i in range(count - 1)]
    backward = [(target, source) for source, target in forward]
    low = lax.ppermute(
        lax.slice_in_dim(block, block.shape[dim] - 1, None, axis=dim), axis, forward
    )
    high = lax.ppermute(lax.slice_in_dim(block, 0, 1, axis=dim), axis, backward)
    return jnp.concatenate([low, block, high], axis=dim)


def halve(x, dim, axis, flip):
    size = x.shape[dim] // 2
    bit = (lax.axis_index(axis) // flip) % 2
    keep = lax.dynamic_slice_in_dim(x, bit * size, size, axis=dim)
    give = lax.dynamic_slice_in_dim(x, (1 - bit) * size, size, axis=dim)
    pairs = [(i, i ^ flip) for i in range(lax.axis_size(axis))]
    return keep + lax.ppermute(give, axis, pairs)


def bits_of(n):
    count = n.bit_length() - 1
    assert 1 << count == n
    return count


def owner_pairs(order, sizes):
    names = ("group", "dp", "space")
    count = sizes["group"] * sizes["dp"] * sizes["space"]
    pairs = []
    for linear in range(count):
        where = {
            "group": linear // (sizes["dp"] * sizes["space"]),
            "dp": (linear // sizes["space"]) % sizes["dp"],
            "space": linear % sizes["space"],
        }
        chunk = 0
        for axis, flip in order:
            chunk = chunk * 2 + (where[axis] // flip) % 2
        pairs.append((linear, chunk))
    return names, pairs


def reduce_weight_grad(total):
    ntaps, chans, outs = total.shape
    sizes = {name: lax.axis_size(name) for name in ("group", "dp", "space")}
    ng = sizes["group"]
    across = 4 if ng % 4 == 0 else ng
    down = ng // across
    assert chans * sizes["space"] == ng * sizes["dp"] * sizes["space"]
    first = ("space", 1)
    ys = [("group", across << b) for b in range(bits_of(down))]
    xs = [("group", 1 << b) for b in range(bits_of(across))]
    ds = [("dp", 1 << b) for b in range(bits_of(sizes["dp"]))]
    assert sizes["space"] == 2
    lanes = (ds, xs, ys)
    spread = [lane[0] for lane in lanes]
    rest = [key for lane in (xs, ys, ds) for key in lane[1:]]
    per = ntaps // len(lanes)
    parts, orders = [], []
    for n in range(len(lanes)):
        order = [first] + spread[n:] + spread[:n]
        part = total[n * per : (n + 1) * per]
        for axis, flip in order[1:]:
            part = halve(part, 1, axis, flip)
        parts.append(part)
        orders.append(order + rest)
    joined = jnp.stack(parts)
    for axis, flip in rest:
        joined = halve(joined, 2, axis, flip)
    parts = []
    for n, order in enumerate(orders):
        names, pairs = owner_pairs(order, sizes)
        parts.append(lax.ppermute(joined[n], names, pairs).reshape(per, outs))
    return jnp.concatenate(parts, axis=0)


def clip_tables(clip_id, frames):
    ids = lax.all_gather(clip_id, "group", axis=1, tiled=True)
    total = ids.shape[1]
    index = jnp.arange(total, dtype=jnp.int32)[None, :]
    prev = jnp.concatenate([jnp.full_like(ids[:, :1], -1), ids[:, :-1]], axis=1)
    boundary = ids != prev
    start = lax.cummax(jnp.where(boundary, index, 0), axis=1)
    position = index - start
    ext = jnp.concatenate([jnp.full_like(ids[:, :2], -1), ids], axis=1)
    same = jnp.stack([ext[:, 2 - k : 2 - k + total] == ids for k in range(3)], axis=0)
    first = lax.axis_index("group") * frames
    pos_pad = jnp.concatenate([jnp.zeros_like(position[:, :2]), position], axis=1)
    pos_wide = lax.dynamic_slice_in_dim(pos_pad, first, frames + 2, axis=1)
    same_pad = jnp.concatenate([same, jnp.zeros_like(same[:, :, :2])], axis=2)
    own = lax.dynamic_slice_in_dim(same_pad, first, frames + 2, axis=2)
    fwd = own[:, :, :frames]
    bwd = jnp.stack([own[k, :, k : k + frames] for k in range(3)], axis=0)
    return pos_wide, fwd, bwd


def local(video, cotangent, weight, clip_id):
    frames = video.shape[1]
    rows = video.shape[2]
    cols = video.shape[3]
    chans = video.shape[4]
    past = passed_along(lax.slice_in_dim(video, frames - 2, None, axis=1), "group", 1)
    vwide = row_halo(jnp.concatenate([past, video], axis=1), "space", 2)
    pos_wide, same_fwd, same_bwd = clip_tables(clip_id, frames)
    omega = 0.37 * (jnp.arange(chans) % 8 + 1).astype(jnp.float32)
    embed = jnp.sin(pos_wide.astype(jnp.float32)[:, :, None] * omega)
    shifted = (vwide.astype(jnp.float32) + embed[:, :, None, None, :]).astype(jnp.bfloat16)
    row = jnp.arange(rows + 2)
    where_s = lax.axis_index("space")
    inside = ((row > 0) | (where_s > 0)) & ((row < rows + 1) | (where_s < lax.axis_size("space") - 1))
    shifted = jnp.where(inside[None, None, :, None, None], shifted, jnp.zeros_like(shifted))
    maskf = same_fwd.astype(jnp.float32)
    widened = jnp.pad(shifted, ((0, 0), (0, 0), (0, 0), (1, 1), (0, 0)))
    stacked = jnp.concatenate([widened[:, :, :, b : b + cols] for b in range(3)], axis=4)
    taps = weight.reshape(3, 3, 3 * chans, chans)
    pre = jnp.zeros(video.shape, jnp.float32)
    for k in range(3):
        part = jnp.zeros(video.shape, jnp.float32)
        for a in range(3):
            block = stacked[:, 2 - k : 2 - k + frames, a : a + rows]
            part = part + jnp.einsum(
                "sfhwk,kc->sfhwc", block, taps[k, a], preferred_element_type=jnp.float32
            )
        pre = pre + part * maskf[k][:, :, None, None, None]
    sigma = jax.nn.sigmoid(pre)
    activation = (pre * sigma).astype(jnp.bfloat16)
    delta = (cotangent.astype(jnp.float32) * sigma * (1.0 + pre * (1.0 - sigma))).astype(
        jnp.bfloat16
    )
    ahead = passed_along(lax.slice_in_dim(delta, 0, 2, axis=1), "group", -1)
    gwide = row_halo(jnp.concatenate([delta, ahead], axis=1), "space", 2)
    swap = [(0, 1), (1, 0)]
    half = chans // 2
    both = jnp.concatenate([shifted, lax.ppermute(shifted, "space", swap)], axis=0)
    both = lax.dynamic_slice_in_dim(both, lax.axis_index("space") * half, half, axis=4)
    both = jnp.pad(both, ((0, 0), (0, 0), (0, 0), (1, 1), (0, 0)))
    bstack = jnp.concatenate([both[:, :, :, b : b + cols] for b in range(3)], axis=4)
    bdelta = jnp.concatenate([delta, lax.ppermute(delta, "space", swap)], axis=0)
    terms = []
    for k in range(3):
        masked = bdelta * same_fwd[k].astype(jnp.bfloat16)[:, :, None, None, None]
        for a in range(3):
            block = bstack[:, 2 - k : 2 - k + frames, a : a + rows]
            terms.append(
                jnp.einsum("sfhwk,sfhwc->kc", block, masked, preferred_element_type=jnp.float32)
            )
    total = jnp.stack(terms).reshape(27, half, chans)
    reduced = reduce_weight_grad(total)
    gwide = jnp.pad(gwide, ((0, 0), (0, 0), (0, 0), (1, 1), (0, 0)))
    gstack = jnp.concatenate([gwide[:, :, :, 2 - b : 2 - b + cols] for b in range(3)], axis=4)
    back = (
        weight.reshape(3, 3, 3, chans, chans)
        .transpose(0, 1, 2, 4, 3)
        .reshape(3, 3, 3 * chans, chans)
    )
    grad = jnp.zeros(video.shape, jnp.float32)
    for k in range(3):
        part = jnp.zeros(video.shape, jnp.float32)
        for a in range(3):
            block = gstack[:, k : k + frames, 2 - a : 2 - a + rows]
            part = part + jnp.einsum(
                "sfhwk,kc->sfhwc", block, back[k, a], preferred_element_type=jnp.float32
            )
        grad = grad + part * same_bwd[k].astype(jnp.float32)[:, :, None, None, None]
    return (activation, grad.astype(jnp.bfloat16), reduced)


def solution(mesh):
    placed = (
        P("dp", "group", "space", None, None),
        P("dp", "group", "space", None, None),
        P(),
        P("dp", "group"),
    )
    return jax.shard_map(
        local,
        mesh=mesh,
        in_specs=placed,
        out_specs=(
            P("dp", "group", "space", None, None),
            P("dp", "group", "space", None, None),
            P(None, ("group", "dp", "space")),
        ),
        check_vma=False,
    )
```

```python
import jax
import jax.numpy as jnp
from jax import lax
from jax.sharding import PartitionSpec as P


def passed_along(value, axis, by):
    length = lax.axis_size(axis)
    pairs = [(i, i + by) for i in range(length) if 0 <= i + by < length]
    return lax.ppermute(value, axis, pairs)


def row_halo(block, axis, dim):
    count = lax.axis_size(axis)
    forward = [(i, i + 1) for i in range(count - 1)]
    backward = [(target, source) for source, target in forward]
    low = lax.ppermute(
        lax.slice_in_dim(block, block.shape[dim] - 1, None, axis=dim), axis, forward
    )
    high = lax.ppermute(lax.slice_in_dim(block, 0, 1, axis=dim), axis, backward)
    return jnp.concatenate([low, block, high], axis=dim)


def halve(x, dim, axis, flip):
    size = x.shape[dim] // 2
    bit = (lax.axis_index(axis) // flip) % 2
    keep = lax.dynamic_slice_in_dim(x, bit * size, size, axis=dim)
    give = lax.dynamic_slice_in_dim(x, (1 - bit) * size, size, axis=dim)
    pairs = [(i, i ^ flip) for i in range(lax.axis_size(axis))]
    return keep + lax.ppermute(give, axis, pairs)


def bits_of(n):
    count = n.bit_length() - 1
    assert 1 << count == n
    return count


def owner_pairs(order, sizes, flipped=None):
    names = ("group", "dp", "space")
    count = sizes["group"] * sizes["dp"] * sizes["space"]
    pairs = []
    for linear in range(count):
        where = {
            "group": linear // (sizes["dp"] * sizes["space"]),
            "dp": (linear // sizes["space"]) % sizes["dp"],
            "space": linear % sizes["space"],
        }
        if flipped is not None:
            where[flipped[0]] ^= flipped[1]
        chunk = 0
        for axis, flip in order:
            chunk = chunk * 2 + (where[axis] // flip) % 2
        pairs.append((linear, chunk))
    return names, pairs


def reduce_weight_grad(total):
    ntaps, chans, outs = total.shape
    sizes = {name: lax.axis_size(name) for name in ("group", "dp", "space")}
    ng = sizes["group"]
    across = 4 if ng % 4 == 0 else ng
    down = ng // across
    assert chans * sizes["space"] == ng * sizes["dp"] * sizes["space"]
    first = ("space", 1)
    ys = [("group", across << b) for b in range(bits_of(down))]
    xs = [("group", 1 << b) for b in range(bits_of(across))]
    ds = [("dp", 1 << b) for b in range(bits_of(sizes["dp"]))]
    assert sizes["space"] == 2
    lanes = (ds, xs, ys)
    spread = [lane[0] for lane in lanes]
    rest = [key for lane in (xs, ys, ds) for key in lane[1:]]
    per = ntaps // len(lanes)
    parts, orders = [], []
    for n in range(len(lanes)):
        order = [first] + spread[n:] + spread[:n]
        part = total[n * per : (n + 1) * per]
        for axis, flip in order[1:]:
            part = halve(part, 1, axis, flip)
        parts.append(part)
        orders.append(order + rest)
    joined = jnp.stack(parts)
    for axis, flip in rest[:-1]:
        joined = halve(joined, 2, axis, flip)
    last = rest[-1]
    bit = (lax.axis_index(last[0]) // last[1]) % 2
    size = joined.shape[2] // 2
    keep = lax.dynamic_slice_in_dim(joined, bit * size, size, axis=2)
    give = lax.dynamic_slice_in_dim(joined, (1 - bit) * size, size, axis=2)
    parts = []
    for n, order in enumerate(orders):
        names, pairs = owner_pairs(order, sizes)
        _, cross = owner_pairs(order, sizes, last)
        got = lax.ppermute(keep[n], names, pairs) + lax.ppermute(give[n], names, cross)
        parts.append(got.reshape(per, outs))
    return jnp.concatenate(parts, axis=0)


def clip_tables(clip_id, frames):
    ids = lax.all_gather(clip_id, "group", axis=1, tiled=True)
    total = ids.shape[1]
    index = jnp.arange(total, dtype=jnp.int32)[None, :]
    prev = jnp.concatenate([jnp.full_like(ids[:, :1], -1), ids[:, :-1]], axis=1)
    boundary = ids != prev
    start = lax.cummax(jnp.where(boundary, index, 0), axis=1)
    position = index - start
    ext = jnp.concatenate([jnp.full_like(ids[:, :2], -1), ids], axis=1)
    same = jnp.stack([ext[:, 2 - k : 2 - k + total] == ids for k in range(3)], axis=0)
    first = lax.axis_index("group") * frames
    pos_pad = jnp.concatenate([jnp.zeros_like(position[:, :2]), position], axis=1)
    pos_wide = lax.dynamic_slice_in_dim(pos_pad, first, frames + 2, axis=1)
    same_pad = jnp.concatenate([same, jnp.zeros_like(same[:, :, :2])], axis=2)
    own = lax.dynamic_slice_in_dim(same_pad, first, frames + 2, axis=2)
    fwd = own[:, :, :frames]
    bwd = jnp.stack([own[k, :, k : k + frames] for k in range(3)], axis=0)
    return pos_wide, fwd, bwd


def local(video, cotangent, weight, clip_id):
    frames = video.shape[1]
    rows = video.shape[2]
    cols = video.shape[3]
    chans = video.shape[4]
    past = passed_along(lax.slice_in_dim(video, frames - 2, None, axis=1), "group", 1)
    vwide = row_halo(jnp.concatenate([past, video], axis=1), "space", 2)
    pos_wide, same_fwd, same_bwd = clip_tables(clip_id, frames)
    omega = 0.37 * (jnp.arange(chans) % 8 + 1).astype(jnp.float32)
    embed = jnp.sin(pos_wide.astype(jnp.float32)[:, :, None] * omega)
    shifted = (vwide.astype(jnp.float32) + embed[:, :, None, None, :]).astype(jnp.bfloat16)
    row = jnp.arange(rows + 2)
    where_s = lax.axis_index("space")
    inside = ((row > 0) | (where_s > 0)) & ((row < rows + 1) | (where_s < lax.axis_size("space") - 1))
    shifted = jnp.where(inside[None, None, :, None, None], shifted, jnp.zeros_like(shifted))
    maskf = same_fwd.astype(jnp.float32)
    widened = jnp.pad(shifted, ((0, 0), (0, 0), (0, 0), (1, 1), (0, 0)))
    stacked = jnp.concatenate([widened[:, :, :, b : b + cols] for b in range(3)], axis=4)
    taps = weight.reshape(3, 3, 3 * chans, chans)
    pre = jnp.zeros(video.shape, jnp.float32)
    for k in range(3):
        part = jnp.zeros(video.shape, jnp.float32)
        for a in range(3):
            block = stacked[:, 2 - k : 2 - k + frames, a : a + rows]
            part = part + jnp.einsum(
                "sfhwk,kc->sfhwc", block, taps[k, a], preferred_element_type=jnp.float32
            )
        pre = pre + part * maskf[k][:, :, None, None, None]
    sigma = jax.nn.sigmoid(pre)
    activation = (pre * sigma).astype(jnp.bfloat16)
    delta = (cotangent.astype(jnp.float32) * sigma * (1.0 + pre * (1.0 - sigma))).astype(
        jnp.bfloat16
    )
    ahead = passed_along(lax.slice_in_dim(delta, 0, 2, axis=1), "group", -1)
    gwide = row_halo(jnp.concatenate([delta, ahead], axis=1), "space", 2)
    swap = [(0, 1), (1, 0)]
    half = chans // 2
    both = jnp.concatenate([shifted, lax.ppermute(shifted, "space", swap)], axis=0)
    both = lax.dynamic_slice_in_dim(both, lax.axis_index("space") * half, half, axis=4)
    both = jnp.pad(both, ((0, 0), (0, 0), (0, 0), (1, 1), (0, 0)))
    bstack = jnp.concatenate([both[:, :, :, b : b + cols] for b in range(3)], axis=4)
    bdelta = jnp.concatenate([delta, lax.ppermute(delta, "space", swap)], axis=0)
    terms = []
    for k in range(3):
        masked = bdelta * same_fwd[k].astype(jnp.bfloat16)[:, :, None, None, None]
        for a in range(3):
            block = bstack[:, 2 - k : 2 - k + frames, a : a + rows]
            terms.append(
                jnp.einsum("sfhwk,sfhwc->kc", block, masked, preferred_element_type=jnp.float32)
            )
    total = jnp.stack(terms).reshape(27, half, chans)
    reduced = reduce_weight_grad(total)
    gwide = jnp.pad(gwide, ((0, 0), (0, 0), (0, 0), (1, 1), (0, 0)))
    gstack = jnp.concatenate([gwide[:, :, :, 2 - b : 2 - b + cols] for b in range(3)], axis=4)
    back = (
        weight.reshape(3, 3, 3, chans, chans)
        .transpose(0, 1, 2, 4, 3)
        .reshape(3, 3, 3 * chans, chans)
    )
    grad = jnp.zeros(video.shape, jnp.float32)
    for k in range(3):
        part = jnp.zeros(video.shape, jnp.float32)
        for a in range(3):
            block = gstack[:, k : k + frames, 2 - a : 2 - a + rows]
            part = part + jnp.einsum(
                "sfhwk,kc->sfhwc", block, back[k, a], preferred_element_type=jnp.float32
            )
        grad = grad + part * same_bwd[k].astype(jnp.float32)[:, :, None, None, None]
    return (activation, grad.astype(jnp.bfloat16), reduced)


def solution(mesh):
    placed = (
        P("dp", "group", "space", None, None),
        P("dp", "group", "space", None, None),
        P(),
        P("dp", "group"),
    )
    return jax.shard_map(
        local,
        mesh=mesh,
        in_specs=placed,
        out_specs=(
            P("dp", "group", "space", None, None),
            P("dp", "group", "space", None, None),
            P(None, ("group", "dp", "space")),
        ),
        check_vma=False,
    )
```

```python
import jax
import jax.numpy as jnp
from jax import lax
from jax.sharding import PartitionSpec as P


GROUP = ("gy", "gx")


def axis_count(axis):
    names = axis if isinstance(axis, tuple) else (axis,)
    count = 1
    for name in names:
        count *= lax.axis_size(name)
    return count


def passed_along(value, axis, by):
    length = axis_count(axis)
    pairs = [(i, i + by) for i in range(length) if 0 <= i + by < length]
    return lax.ppermute(value, axis, pairs)


def row_halo(block, axis, dim):
    count = lax.axis_size(axis)
    forward = [(i, i + 1) for i in range(count - 1)]
    backward = [(target, source) for source, target in forward]
    low = lax.ppermute(
        lax.slice_in_dim(block, block.shape[dim] - 1, None, axis=dim), axis, forward
    )
    high = lax.ppermute(lax.slice_in_dim(block, 0, 1, axis=dim), axis, backward)
    return jnp.concatenate([low, block, high], axis=dim)


def halve(x, dim, axis, flip):
    size = x.shape[dim] // 2
    bit = (lax.axis_index(axis) // flip) % 2
    keep = lax.dynamic_slice_in_dim(x, bit * size, size, axis=dim)
    give = lax.dynamic_slice_in_dim(x, (1 - bit) * size, size, axis=dim)
    pairs = [(i, i ^ flip) for i in range(axis_count(axis))]
    return keep + lax.ppermute(give, axis, pairs)


def bits_of(n):
    count = n.bit_length() - 1
    assert 1 << count == n
    return count


def owner_pairs(order, sizes):
    names = tuple(sizes)
    count = 1
    for name in names:
        count *= sizes[name]
    pairs = []
    for linear in range(count):
        where, rest = {}, linear
        for name in reversed(names):
            where[name] = rest % sizes[name]
            rest //= sizes[name]
        chunk = 0
        for axis, flip in order:
            chunk = chunk * 2 + (where[axis] // flip) % 2
        pairs.append((linear, chunk))
    return names, pairs


def reduce_weight_grad(total):
    ntaps, chans, outs = total.shape
    sizes = {name: lax.axis_size(name) for name in GROUP + ("dp", "space")}
    down, across = sizes["gy"], sizes["gx"]
    assert chans * 2 == down * across * sizes["dp"] * sizes["space"]
    first = ("space", 1)
    ys = [("gy", 1 << b) for b in range(bits_of(down))]
    xs = [("gx", 1 << b) for b in range(bits_of(across))]
    ds = [("dp", 1 << b) for b in range(bits_of(sizes["dp"]))]
    assert sizes["space"] == 2
    lanes = (ds, xs, ys)
    spread = [lane[0] for lane in lanes]
    rest = [key for lane in (xs, ys, ds) for key in lane[1:]]
    per = ntaps // len(lanes)
    parts, orders = [], []
    for n in range(len(lanes)):
        order = [first] + spread[n:] + spread[:n]
        part = total[n * per : (n + 1) * per]
        for axis, flip in order[1:]:
            part = halve(part, 1, axis, flip)
        parts.append(part)
        orders.append(order + rest)
    joined = jnp.stack(parts)
    for axis, flip in rest:
        joined = halve(joined, 2, axis, flip)
    parts = []
    for n, order in enumerate(orders):
        names, pairs = owner_pairs(order, sizes)
        parts.append(lax.ppermute(joined[n], names, pairs).reshape(per, outs))
    return jnp.concatenate(parts, axis=0)


def clip_tables(clip_id, frames):
    ids = lax.all_gather(clip_id, "gx", axis=1, tiled=True)
    ids = lax.all_gather(ids, "gy", axis=1, tiled=True)
    total = ids.shape[1]
    index = jnp.arange(total, dtype=jnp.int32)[None, :]
    prev = jnp.concatenate([jnp.full_like(ids[:, :1], -1), ids[:, :-1]], axis=1)
    boundary = ids != prev
    start = lax.cummax(jnp.where(boundary, index, 0), axis=1)
    position = index - start
    ext = jnp.concatenate([jnp.full_like(ids[:, :2], -1), ids], axis=1)
    same = jnp.stack([ext[:, 2 - k : 2 - k + total] == ids for k in range(3)], axis=0)
    first = lax.axis_index(GROUP) * frames
    pos_pad = jnp.concatenate([jnp.zeros_like(position[:, :2]), position], axis=1)
    pos_wide = lax.dynamic_slice_in_dim(pos_pad, first, frames + 2, axis=1)
    same_pad = jnp.concatenate([same, jnp.zeros_like(same[:, :, :2])], axis=2)
    own = lax.dynamic_slice_in_dim(same_pad, first, frames + 2, axis=2)
    fwd = own[:, :, :frames]
    bwd = jnp.stack([own[k, :, k : k + frames] for k in range(3)], axis=0)
    return pos_wide, fwd, bwd


def local(video, cotangent, weight, clip_id):
    frames = video.shape[1]
    rows = video.shape[2]
    cols = video.shape[3]
    chans = video.shape[4]
    past = passed_along(lax.slice_in_dim(video, frames - 2, None, axis=1), GROUP, 1)
    vwide = row_halo(jnp.concatenate([past, video], axis=1), "space", 2)
    pos_wide, same_fwd, same_bwd = clip_tables(clip_id, frames)
    omega = 0.37 * (jnp.arange(chans) % 8 + 1).astype(jnp.float32)
    embed = jnp.sin(pos_wide.astype(jnp.float32)[:, :, None] * omega)
    shifted = (vwide.astype(jnp.float32) + embed[:, :, None, None, :]).astype(jnp.bfloat16)
    row = jnp.arange(rows + 2)
    where_s = lax.axis_index("space")
    inside = ((row > 0) | (where_s > 0)) & ((row < rows + 1) | (where_s < lax.axis_size("space") - 1))
    shifted = jnp.where(inside[None, None, :, None, None], shifted, jnp.zeros_like(shifted))
    maskf = same_fwd.astype(jnp.float32)
    widened = jnp.pad(shifted, ((0, 0), (0, 0), (0, 0), (1, 1), (0, 0)))
    stacked = jnp.concatenate([widened[:, :, :, b : b + cols] for b in range(3)], axis=4)
    taps = weight.reshape(3, 3, 3 * chans, chans)
    pre = jnp.zeros(video.shape, jnp.float32)
    for k in range(3):
        part = jnp.zeros(video.shape, jnp.float32)
        for a in range(3):
            block = stacked[:, 2 - k : 2 - k + frames, a : a + rows]
            part = part + jnp.einsum(
                "sfhwk,kc->sfhwc", block, taps[k, a], preferred_element_type=jnp.float32
            )
        pre = pre + part * maskf[k][:, :, None, None, None]
    sigma = jax.nn.sigmoid(pre)
    activation = (pre * sigma).astype(jnp.bfloat16)
    delta = (cotangent.astype(jnp.float32) * sigma * (1.0 + pre * (1.0 - sigma))).astype(
        jnp.bfloat16
    )
    ahead = passed_along(lax.slice_in_dim(delta, 0, 2, axis=1), GROUP, -1)
    gwide = row_halo(jnp.concatenate([delta, ahead], axis=1), "space", 2)
    swap = [(0, 1), (1, 0)]
    half = chans // 2
    both = jnp.concatenate([shifted, lax.ppermute(shifted, "space", swap)], axis=0)
    both = lax.dynamic_slice_in_dim(both, lax.axis_index("space") * half, half, axis=4)
    both = jnp.pad(both, ((0, 0), (0, 0), (0, 0), (1, 1), (0, 0)))
    bstack = jnp.concatenate([both[:, :, :, b : b + cols] for b in range(3)], axis=4)
    bdelta = jnp.concatenate([delta, lax.ppermute(delta, "space", swap)], axis=0)
    terms = []
    for k in range(3):
        masked = bdelta * same_fwd[k].astype(jnp.bfloat16)[:, :, None, None, None]
        for a in range(3):
            block = bstack[:, 2 - k : 2 - k + frames, a : a + rows]
            terms.append(
                jnp.einsum("sfhwk,sfhwc->kc", block, masked, preferred_element_type=jnp.float32)
            )
    total = jnp.stack(terms).reshape(27, half, chans)
    reduced = reduce_weight_grad(total)
    gwide = jnp.pad(gwide, ((0, 0), (0, 0), (0, 0), (1, 1), (0, 0)))
    gstack = jnp.concatenate([gwide[:, :, :, 2 - b : 2 - b + cols] for b in range(3)], axis=4)
    back = (
        weight.reshape(3, 3, 3, chans, chans)
        .transpose(0, 1, 2, 4, 3)
        .reshape(3, 3, 3 * chans, chans)
    )
    grad = jnp.zeros(video.shape, jnp.float32)
    for k in range(3):
        part = jnp.zeros(video.shape, jnp.float32)
        for a in range(3):
            block = gstack[:, k : k + frames, 2 - a : 2 - a + rows]
            part = part + jnp.einsum(
                "sfhwk,kc->sfhwc", block, back[k, a], preferred_element_type=jnp.float32
            )
        grad = grad + part * same_bwd[k].astype(jnp.float32)[:, :, None, None, None]
    return (activation, grad.astype(jnp.bfloat16), reduced)


def solution(mesh):
    whole = mesh.devices
    across = 4 if whole.shape[0] % 4 == 0 else whole.shape[0]
    fine = jax.sharding.Mesh(
        whole.reshape((whole.shape[0] // across, across) + whole.shape[1:]), GROUP + ("dp", "space")
    )
    video_spec = P("dp", GROUP, "space", None, None)
    return jax.shard_map(
        local,
        mesh=fine,
        in_specs=(video_spec, video_spec, P(), P("dp", GROUP)),
        out_specs=(video_spec, video_spec, P(None, GROUP + ("dp", "space"))),
        check_vma=False,
    )
```

```python
import jax
import jax.numpy as jnp
from jax import lax
from jax.sharding import PartitionSpec as P


def passed_along(value, axis, by):
    length = lax.axis_size(axis)
    pairs = [(i, i + by) for i in range(length) if 0 <= i + by < length]
    return lax.ppermute(value, axis, pairs)


def row_halo(block, axis, dim):
    count = lax.axis_size(axis)
    forward = [(i, i + 1) for i in range(count - 1)]
    backward = [(target, source) for source, target in forward]
    low = lax.ppermute(
        lax.slice_in_dim(block, block.shape[dim] - 1, None, axis=dim), axis, forward
    )
    high = lax.ppermute(lax.slice_in_dim(block, 0, 1, axis=dim), axis, backward)
    return jnp.concatenate([low, block, high], axis=dim)


def halve(x, dim, axis, flip):
    size = x.shape[dim] // 2
    bit = (lax.axis_index(axis) // flip) % 2
    keep = lax.dynamic_slice_in_dim(x, bit * size, size, axis=dim)
    give = lax.dynamic_slice_in_dim(x, (1 - bit) * size, size, axis=dim)
    pairs = [(i, i ^ flip) for i in range(lax.axis_size(axis))]
    return keep + lax.ppermute(give, axis, pairs)


def bits_of(n):
    count = n.bit_length() - 1
    assert 1 << count == n
    return count


def owner_pairs(order, sizes):
    names = ("group", "dp", "space")
    count = sizes["group"] * sizes["dp"] * sizes["space"]
    pairs = []
    for linear in range(count):
        where = {
            "group": linear // (sizes["dp"] * sizes["space"]),
            "dp": (linear // sizes["space"]) % sizes["dp"],
            "space": linear % sizes["space"],
        }
        chunk = 0
        for axis, flip in order:
            chunk = chunk * 2 + (where[axis] // flip) % 2
        pairs.append((linear, chunk))
    return names, pairs


def reduce_weight_grad(total):
    ntaps, chans, outs = total.shape
    sizes = {name: lax.axis_size(name) for name in ("group", "dp", "space")}
    ng = sizes["group"]
    across = 4 if ng % 4 == 0 else ng
    down = ng // across
    assert chans * sizes["space"] == ng * sizes["dp"] * sizes["space"]
    first = ("space", 1)
    ys = [("group", across << b) for b in range(bits_of(down))]
    xs = [("group", 1 << b) for b in range(bits_of(across))]
    ds = [("dp", 1 << b) for b in range(bits_of(sizes["dp"]))]
    assert sizes["space"] == 2
    lanes = (ds, xs, ys)
    spread = [lane[0] for lane in lanes]
    rest = [key for lane in (xs, ys, ds) for key in lane[1:]]
    per = ntaps // len(lanes)
    parts, orders = [], []
    for n in range(len(lanes)):
        order = [first] + spread[n:] + spread[:n]
        part = total[n * per : (n + 1) * per]
        for axis, flip in order[1:]:
            part = halve(part, 1, axis, flip)
        parts.append(part)
        orders.append(order + rest)
    joined = jnp.stack(parts)
    for axis, flip in rest:
        joined = halve(joined, 2, axis, flip)
    parts = []
    for n, order in enumerate(orders):
        names, pairs = owner_pairs(order, sizes)
        parts.append(lax.ppermute(joined[n], names, pairs).reshape(per, outs))
    return jnp.concatenate(parts, axis=0)


def clip_tables(clip_id, frames):
    ids = lax.all_gather(clip_id, "group", axis=1, tiled=True)
    total = ids.shape[1]
    index = jnp.arange(total, dtype=jnp.int32)[None, :]
    prev = jnp.concatenate([jnp.full_like(ids[:, :1], -1), ids[:, :-1]], axis=1)
    boundary = ids != prev
    start = lax.cummax(jnp.where(boundary, index, 0), axis=1)
    position = index - start
    ext = jnp.concatenate([jnp.full_like(ids[:, :2], -1), ids], axis=1)
    same = jnp.stack([ext[:, 2 - k : 2 - k + total] == ids for k in range(3)], axis=0)
    first = lax.axis_index("group") * frames
    pos_pad = jnp.concatenate([jnp.zeros_like(position[:, :2]), position], axis=1)
    pos_wide = lax.dynamic_slice_in_dim(pos_pad, first, frames + 2, axis=1)
    same_pad = jnp.concatenate([same, jnp.zeros_like(same[:, :, :2])], axis=2)
    own = lax.dynamic_slice_in_dim(same_pad, first, frames + 2, axis=2)
    fwd = own[:, :, :frames]
    bwd = jnp.stack([own[k, :, k : k + frames] for k in range(3)], axis=0)
    return pos_wide, fwd, bwd


def local(video, cotangent, weight, clip_id):
    frames = video.shape[1]
    rows = video.shape[2]
    cols = video.shape[3]
    chans = video.shape[4]
    assert lax.axis_size("space") == 2
    swap = [(0, 1), (1, 0)]
    where_s = lax.axis_index("space")
    tail = lax.slice_in_dim(video, frames - 2, None, axis=1)
    past = passed_along(tail, "group", 1)
    other_now = lax.ppermute(video, "space", swap)
    count = lax.axis_size("group")
    diagonal = [(g * 2 + c, (g + 1) * 2 + 1 - c) for g in range(count - 1) for c in range(2)]
    other_past = lax.ppermute(tail, ("group", "space"), diagonal)
    mine = jnp.concatenate([past, video], axis=1)
    theirs = jnp.concatenate([other_past, other_now], axis=1)
    full = jnp.where(
        where_s == 0,
        jnp.concatenate([mine, theirs], axis=2),
        jnp.concatenate([theirs, mine], axis=2),
    )
    pos_wide, same_fwd, same_bwd = clip_tables(clip_id, frames)
    omega = 0.37 * (jnp.arange(chans) % 8 + 1).astype(jnp.float32)
    embed = jnp.sin(pos_wide.astype(jnp.float32)[:, :, None] * omega)
    whole = (full.astype(jnp.float32) + embed[:, :, None, None, :]).astype(jnp.bfloat16)
    whole = jnp.pad(whole, ((0, 0), (0, 0), (1, 1), (0, 0), (0, 0)))
    shifted = lax.dynamic_slice_in_dim(whole, where_s * rows, rows + 2, axis=2)
    shifted_other = lax.dynamic_slice_in_dim(whole, (1 - where_s) * rows, rows + 2, axis=2)
    maskf = same_fwd.astype(jnp.float32)
    widened = jnp.pad(shifted, ((0, 0), (0, 0), (0, 0), (1, 1), (0, 0)))
    stacked = jnp.concatenate([widened[:, :, :, b : b + cols] for b in range(3)], axis=4)
    taps = weight.reshape(3, 3, 3 * chans, chans)
    pre = jnp.zeros(video.shape, jnp.float32)
    for k in range(3):
        part = jnp.zeros(video.shape, jnp.float32)
        for a in range(3):
            block = stacked[:, 2 - k : 2 - k + frames, a : a + rows]
            part = part + jnp.einsum(
                "sfhwk,kc->sfhwc", block, taps[k, a], preferred_element_type=jnp.float32
            )
        pre = pre + part * maskf[k][:, :, None, None, None]
    sigma = jax.nn.sigmoid(pre)
    activation = (pre * sigma).astype(jnp.bfloat16)
    delta = (cotangent.astype(jnp.float32) * sigma * (1.0 + pre * (1.0 - sigma))).astype(
        jnp.bfloat16
    )
    ahead = passed_along(lax.slice_in_dim(delta, 0, 2, axis=1), "group", -1)
    gwide = row_halo(jnp.concatenate([delta, ahead], axis=1), "space", 2)
    half = chans // 2
    both = jnp.concatenate([shifted, shifted_other], axis=0)
    both = lax.dynamic_slice_in_dim(both, lax.axis_index("space") * half, half, axis=4)
    both = jnp.pad(both, ((0, 0), (0, 0), (0, 0), (1, 1), (0, 0)))
    bstack = jnp.concatenate([both[:, :, :, b : b + cols] for b in range(3)], axis=4)
    bdelta = jnp.concatenate([delta, lax.ppermute(delta, "space", swap)], axis=0)
    terms = []
    for k in range(3):
        masked = bdelta * same_fwd[k].astype(jnp.bfloat16)[:, :, None, None, None]
        for a in range(3):
            block = bstack[:, 2 - k : 2 - k + frames, a : a + rows]
            terms.append(
                jnp.einsum("sfhwk,sfhwc->kc", block, masked, preferred_element_type=jnp.float32)
            )
    total = jnp.stack(terms).reshape(27, half, chans)
    reduced = reduce_weight_grad(total)
    gwide = jnp.pad(gwide, ((0, 0), (0, 0), (0, 0), (1, 1), (0, 0)))
    gstack = jnp.concatenate([gwide[:, :, :, 2 - b : 2 - b + cols] for b in range(3)], axis=4)
    back = (
        weight.reshape(3, 3, 3, chans, chans)
        .transpose(0, 1, 2, 4, 3)
        .reshape(3, 3, 3 * chans, chans)
    )
    grad = jnp.zeros(video.shape, jnp.float32)
    for k in range(3):
        part = jnp.zeros(video.shape, jnp.float32)
        for a in range(3):
            block = gstack[:, k : k + frames, 2 - a : 2 - a + rows]
            part = part + jnp.einsum(
                "sfhwk,kc->sfhwc", block, back[k, a], preferred_element_type=jnp.float32
            )
        grad = grad + part * same_bwd[k].astype(jnp.float32)[:, :, None, None, None]
    return (activation, grad.astype(jnp.bfloat16), reduced)


def solution(mesh):
    placed = (
        P("dp", "group", "space", None, None),
        P("dp", "group", "space", None, None),
        P(),
        P("dp", "group"),
    )
    return jax.shard_map(
        local,
        mesh=mesh,
        in_specs=placed,
        out_specs=(
            P("dp", "group", "space", None, None),
            P("dp", "group", "space", None, None),
            P(None, ("group", "dp", "space")),
        ),
        check_vma=False,
    )
```

```python
import jax
import jax.numpy as jnp
from jax import lax
from jax.sharding import PartitionSpec as P


def passed_along(value, axis, by):
    length = lax.axis_size(axis)
    pairs = [(i, i + by) for i in range(length) if 0 <= i + by < length]
    return lax.ppermute(value, axis, pairs)


def row_halo(block, axis, dim):
    count = lax.axis_size(axis)
    forward = [(i, i + 1) for i in range(count - 1)]
    backward = [(target, source) for source, target in forward]
    low = lax.ppermute(
        lax.slice_in_dim(block, block.shape[dim] - 1, None, axis=dim), axis, forward
    )
    high = lax.ppermute(lax.slice_in_dim(block, 0, 1, axis=dim), axis, backward)
    return jnp.concatenate([low, block, high], axis=dim)


def halve(x, dim, axis, flip):
    size = x.shape[dim] // 2
    bit = (lax.axis_index(axis) // flip) % 2
    keep = lax.dynamic_slice_in_dim(x, bit * size, size, axis=dim)
    give = lax.dynamic_slice_in_dim(x, (1 - bit) * size, size, axis=dim)
    pairs = [(i, i ^ flip) for i in range(lax.axis_size(axis))]
    return keep + lax.ppermute(give, axis, pairs)


def bits_of(n):
    count = n.bit_length() - 1
    assert 1 << count == n
    return count


def owner_pairs(order, sizes):
    names = ("group", "dp", "space")
    count = sizes["group"] * sizes["dp"] * sizes["space"]
    pairs = []
    for linear in range(count):
        where = {
            "group": linear // (sizes["dp"] * sizes["space"]),
            "dp": (linear // sizes["space"]) % sizes["dp"],
            "space": linear % sizes["space"],
        }
        chunk = 0
        for axis, flip in order:
            chunk = chunk * 2 + (where[axis] // flip) % 2
        pairs.append((linear, chunk))
    return names, pairs


def reduce_weight_grad(total):
    ntaps, chans, outs = total.shape
    sizes = {name: lax.axis_size(name) for name in ("group", "dp", "space")}
    ng = sizes["group"]
    across = 4 if ng % 4 == 0 else ng
    down = ng // across
    assert chans * sizes["space"] == ng * sizes["dp"] * sizes["space"]
    first = ("space", 1)
    ys = [("group", across << b) for b in range(bits_of(down))]
    xs = [("group", 1 << b) for b in range(bits_of(across))]
    ds = [("dp", 1 << b) for b in range(bits_of(sizes["dp"]))]
    assert sizes["space"] == 2
    lanes = (ds, xs, ys)
    spread = [lane[0] for lane in lanes]
    rest = [key for lane in (xs, ys, ds) for key in lane[1:]]
    per = ntaps // len(lanes)
    parts, orders = [], []
    for n in range(len(lanes)):
        order = [first] + spread[n:] + spread[:n]
        part = total[n * per : (n + 1) * per]
        for axis, flip in order[1:]:
            part = halve(part, 1, axis, flip)
        parts.append(part)
        orders.append(order + rest)
    joined = jnp.stack(parts)
    for axis, flip in rest:
        joined = halve(joined, 2, axis, flip)
    parts = []
    for n, order in enumerate(orders):
        names, pairs = owner_pairs(order, sizes)
        parts.append(lax.ppermute(joined[n], names, pairs).reshape(per, outs))
    return jnp.concatenate(parts, axis=0)


def clip_tables(clip_id, frames):
    lanes = lax.broadcasted_iota(jnp.int32, clip_id.shape + (128,), 2)
    wide = (clip_id[:, :, None] * 1024 + lanes).astype(jnp.float32)
    ids = lax.all_gather(wide, "group", axis=1, tiled=True)
    ids = jnp.sum(ids, axis=2).astype(jnp.int32)
    ids = (ids - 127 * 64) // (128 * 1024)
    total = ids.shape[1]
    index = jnp.arange(total, dtype=jnp.int32)[None, :]
    prev = jnp.concatenate([jnp.full_like(ids[:, :1], -1), ids[:, :-1]], axis=1)
    boundary = ids != prev
    start = lax.cummax(jnp.where(boundary, index, 0), axis=1)
    position = index - start
    ext = jnp.concatenate([jnp.full_like(ids[:, :2], -1), ids], axis=1)
    same = jnp.stack([ext[:, 2 - k : 2 - k + total] == ids for k in range(3)], axis=0)
    first = lax.axis_index("group") * frames
    pos_pad = jnp.concatenate([jnp.zeros_like(position[:, :2]), position], axis=1)
    pos_wide = lax.dynamic_slice_in_dim(pos_pad, first, frames + 2, axis=1)
    same_pad = jnp.concatenate([same, jnp.zeros_like(same[:, :, :2])], axis=2)
    own = lax.dynamic_slice_in_dim(same_pad, first, frames + 2, axis=2)
    fwd = own[:, :, :frames]
    bwd = jnp.stack([own[k, :, k : k + frames] for k in range(3)], axis=0)
    return pos_wide, fwd, bwd


def local(video, cotangent, weight, clip_id):
    frames = video.shape[1]
    rows = video.shape[2]
    cols = video.shape[3]
    chans = video.shape[4]
    assert lax.axis_size("space") == 2
    swap = [(0, 1), (1, 0)]
    where_s = lax.axis_index("space")
    tail = lax.slice_in_dim(video, frames - 2, None, axis=1)
    past = passed_along(tail, "group", 1)
    other_now = lax.ppermute(video, "space", swap)
    count = lax.axis_size("group")
    diagonal = [(g * 2 + c, (g + 1) * 2 + 1 - c) for g in range(count - 1) for c in range(2)]
    other_past = lax.ppermute(tail, ("group", "space"), diagonal)
    mine = jnp.concatenate([past, video], axis=1)
    theirs = jnp.concatenate([other_past, other_now], axis=1)
    full = jnp.where(
        where_s == 0,
        jnp.concatenate([mine, theirs], axis=2),
        jnp.concatenate([theirs, mine], axis=2),
    )
    pos_wide, same_fwd, same_bwd = clip_tables(clip_id, frames)
    omega = 0.37 * (jnp.arange(chans) % 8 + 1).astype(jnp.float32)
    embed = jnp.sin(pos_wide.astype(jnp.float32)[:, :, None] * omega)
    whole = (full.astype(jnp.float32) + embed[:, :, None, None, :]).astype(jnp.bfloat16)
    whole = jnp.pad(whole, ((0, 0), (0, 0), (1, 1), (0, 0), (0, 0)))
    shifted = lax.dynamic_slice_in_dim(whole, where_s * rows, rows + 2, axis=2)
    shifted_other = lax.dynamic_slice_in_dim(whole, (1 - where_s) * rows, rows + 2, axis=2)
    maskf = same_fwd.astype(jnp.float32)
    widened = jnp.pad(shifted, ((0, 0), (0, 0), (0, 0), (1, 1), (0, 0)))
    stacked = jnp.concatenate([widened[:, :, :, b : b + cols] for b in range(3)], axis=4)
    taps = weight.reshape(3, 3, 3 * chans, chans)
    pre = jnp.zeros(video.shape, jnp.float32)
    for k in range(3):
        part = jnp.zeros(video.shape, jnp.float32)
        for a in range(3):
            block = stacked[:, 2 - k : 2 - k + frames, a : a + rows]
            part = part + jnp.einsum(
                "sfhwk,kc->sfhwc", block, taps[k, a], preferred_element_type=jnp.float32
            )
        pre = pre + part * maskf[k][:, :, None, None, None]
    sigma = jax.nn.sigmoid(pre)
    activation = (pre * sigma).astype(jnp.bfloat16)
    delta = (cotangent.astype(jnp.float32) * sigma * (1.0 + pre * (1.0 - sigma))).astype(
        jnp.bfloat16
    )
    ahead = passed_along(lax.slice_in_dim(delta, 0, 2, axis=1), "group", -1)
    gwide = row_halo(jnp.concatenate([delta, ahead], axis=1), "space", 2)
    half = chans // 2
    both = jnp.concatenate([shifted, shifted_other], axis=0)
    both = lax.dynamic_slice_in_dim(both, lax.axis_index("space") * half, half, axis=4)
    both = jnp.pad(both, ((0, 0), (0, 0), (0, 0), (1, 1), (0, 0)))
    bstack = jnp.concatenate([both[:, :, :, b : b + cols] for b in range(3)], axis=4)
    bdelta = jnp.concatenate([delta, lax.ppermute(delta, "space", swap)], axis=0)
    terms = []
    for k in range(3):
        masked = bdelta * same_fwd[k].astype(jnp.bfloat16)[:, :, None, None, None]
        for a in range(3):
            block = bstack[:, 2 - k : 2 - k + frames, a : a + rows]
            terms.append(
                jnp.einsum("sfhwk,sfhwc->kc", block, masked, preferred_element_type=jnp.float32)
            )
    total = jnp.stack(terms).reshape(27, half, chans)
    reduced = reduce_weight_grad(total)
    gwide = jnp.pad(gwide, ((0, 0), (0, 0), (0, 0), (1, 1), (0, 0)))
    gstack = jnp.concatenate([gwide[:, :, :, 2 - b : 2 - b + cols] for b in range(3)], axis=4)
    back = (
        weight.reshape(3, 3, 3, chans, chans)
        .transpose(0, 1, 2, 4, 3)
        .reshape(3, 3, 3 * chans, chans)
    )
    grad = jnp.zeros(video.shape, jnp.float32)
    for k in range(3):
        part = jnp.zeros(video.shape, jnp.float32)
        for a in range(3):
            block = gstack[:, k : k + frames, 2 - a : 2 - a + rows]
            part = part + jnp.einsum(
                "sfhwk,kc->sfhwc", block, back[k, a], preferred_element_type=jnp.float32
            )
        grad = grad + part * same_bwd[k].astype(jnp.float32)[:, :, None, None, None]
    return (activation, grad.astype(jnp.bfloat16), reduced)


def solution(mesh):
    placed = (
        P("dp", "group", "space", None, None),
        P("dp", "group", "space", None, None),
        P(),
        P("dp", "group"),
    )
    return jax.shard_map(
        local,
        mesh=mesh,
        in_specs=placed,
        out_specs=(
            P("dp", "group", "space", None, None),
            P("dp", "group", "space", None, None),
            P(None, ("group", "dp", "space")),
        ),
        check_vma=False,
    )
```

```python
import jax
import jax.numpy as jnp
from jax import lax
from jax.sharding import PartitionSpec as P


def passed_along(value, axis, by):
    length = lax.axis_size(axis)
    pairs = [(i, i + by) for i in range(length) if 0 <= i + by < length]
    return lax.ppermute(value, axis, pairs)


def row_halo(block, axis, dim):
    count = lax.axis_size(axis)
    forward = [(i, i + 1) for i in range(count - 1)]
    backward = [(target, source) for source, target in forward]
    low = lax.ppermute(
        lax.slice_in_dim(block, block.shape[dim] - 1, None, axis=dim), axis, forward
    )
    high = lax.ppermute(lax.slice_in_dim(block, 0, 1, axis=dim), axis, backward)
    return jnp.concatenate([low, block, high], axis=dim)


def halve(x, dim, axis, flip):
    size = x.shape[dim] // 2
    bit = (lax.axis_index(axis) // flip) % 2
    keep = lax.dynamic_slice_in_dim(x, bit * size, size, axis=dim)
    give = lax.dynamic_slice_in_dim(x, (1 - bit) * size, size, axis=dim)
    pairs = [(i, i ^ flip) for i in range(lax.axis_size(axis))]
    return keep + lax.ppermute(give, axis, pairs)


def bits_of(n):
    count = n.bit_length() - 1
    assert 1 << count == n
    return count


def owner_pairs(order, sizes):
    names = ("group", "dp", "space")
    count = sizes["group"] * sizes["dp"] * sizes["space"]
    pairs = []
    for linear in range(count):
        where = {
            "group": linear // (sizes["dp"] * sizes["space"]),
            "dp": (linear // sizes["space"]) % sizes["dp"],
            "space": linear % sizes["space"],
        }
        chunk = 0
        for axis, flip in order:
            chunk = chunk * 2 + (where[axis] // flip) % 2
        pairs.append((linear, chunk))
    return names, pairs


def reduce_weight_grad(total):
    ntaps, chans, outs = total.shape
    sizes = {name: lax.axis_size(name) for name in ("group", "dp", "space")}
    ng = sizes["group"]
    across = 4 if ng % 4 == 0 else ng
    down = ng // across
    assert chans * sizes["space"] == ng * sizes["dp"] * sizes["space"]
    first = ("space", 1)
    ys = [("group", across << b) for b in range(bits_of(down))]
    xs = [("group", 1 << b) for b in range(bits_of(across))]
    ds = [("dp", 1 << b) for b in range(bits_of(sizes["dp"]))]
    assert sizes["space"] == 2
    lanes = (ds, xs, ys)
    spread = [lane[0] for lane in lanes]
    rest = [key for lane in (xs, ys, ds) for key in lane[1:]]
    per = ntaps // len(lanes)
    parts, orders = [], []
    for n in range(len(lanes)):
        order = [first] + spread[n:] + spread[:n]
        part = total[n * per : (n + 1) * per]
        for axis, flip in order[1:]:
            part = halve(part, 1, axis, flip)
        parts.append(part)
        orders.append(order + rest)
    joined = jnp.stack(parts)
    for axis, flip in rest:
        joined = halve(joined, 2, axis, flip)
    parts = []
    for n, order in enumerate(orders):
        names, pairs = owner_pairs(order, sizes)
        parts.append(lax.ppermute(joined[n], names, pairs).reshape(per, outs))
    return jnp.concatenate(parts, axis=0)


def clip_tables(clip_id, frames):
    ids = lax.all_gather(clip_id, "group", axis=1, tiled=True)
    total = ids.shape[1]
    index = jnp.arange(total, dtype=jnp.int32)[None, :]
    prev = jnp.concatenate([jnp.full_like(ids[:, :1], -1), ids[:, :-1]], axis=1)
    boundary = ids != prev
    start = lax.cummax(jnp.where(boundary, index, 0), axis=1)
    position = index - start
    ext = jnp.concatenate([jnp.full_like(ids[:, :2], -1), ids], axis=1)
    same = jnp.stack([ext[:, 2 - k : 2 - k + total] == ids for k in range(3)], axis=0)
    first = lax.axis_index("group") * frames
    pos_pad = jnp.concatenate([jnp.zeros_like(position[:, :2]), position], axis=1)
    pos_wide = lax.dynamic_slice_in_dim(pos_pad, first, frames + 2, axis=1)
    same_pad = jnp.concatenate([same, jnp.zeros_like(same[:, :, :2])], axis=2)
    own = lax.dynamic_slice_in_dim(same_pad, first, frames + 2, axis=2)
    fwd = own[:, :, :frames]
    bwd = jnp.stack([own[k, :, k : k + frames] for k in range(3)], axis=0)
    return pos_wide, fwd, bwd


def local(video, cotangent, weight, clip_id):
    frames = video.shape[1]
    rows = video.shape[2]
    cols = video.shape[3]
    chans = video.shape[4]
    assert lax.axis_size("space") == 2
    swap = [(0, 1), (1, 0)]
    where_s = lax.axis_index("space")
    tail = lax.slice_in_dim(video, frames - 2, None, axis=1)
    past = passed_along(tail, "group", 1)
    other_now = lax.ppermute(video, "space", swap)
    count = lax.axis_size("group")
    diagonal = [(g * 2 + c, (g + 1) * 2 + 1 - c) for g in range(count - 1) for c in range(2)]
    other_past = lax.ppermute(tail, ("group", "space"), diagonal)
    mine = jnp.concatenate([past, video], axis=1)
    theirs = jnp.concatenate([other_past, other_now], axis=1)
    full = jnp.where(
        where_s == 0,
        jnp.concatenate([mine, theirs], axis=2),
        jnp.concatenate([theirs, mine], axis=2),
    )
    pos_wide, same_fwd, same_bwd = clip_tables(clip_id, frames)
    omega = 0.37 * (jnp.arange(chans) % 8 + 1).astype(jnp.float32)
    embed = jnp.sin(pos_wide.astype(jnp.float32)[:, :, None] * omega)
    whole = (full.astype(jnp.float32) + embed[:, :, None, None, :]).astype(jnp.bfloat16)
    whole = jnp.pad(whole, ((0, 0), (0, 0), (1, 1), (0, 0), (0, 0)))
    shifted = lax.dynamic_slice_in_dim(whole, where_s * rows, rows + 2, axis=2)
    shifted_other = lax.dynamic_slice_in_dim(whole, (1 - where_s) * rows, rows + 2, axis=2)
    maskf = same_fwd.astype(jnp.float32)
    widened = jnp.pad(shifted, ((0, 0), (0, 0), (0, 0), (1, 1), (0, 0)))
    stacked = jnp.concatenate([widened[:, :, :, b : b + cols] for b in range(3)], axis=4)
    taps = weight.reshape(3, 3, 3 * chans, chans)
    pre = jnp.zeros(video.shape, jnp.float32)
    for k in range(3):
        part = jnp.zeros(video.shape, jnp.float32)
        for a in range(3):
            block = stacked[:, 2 - k : 2 - k + frames, a : a + rows]
            part = part + jnp.einsum(
                "sfhwk,kc->sfhwc", block, taps[k, a], preferred_element_type=jnp.float32
            )
        pre = pre + part * maskf[k][:, :, None, None, None]
    sigma = jax.nn.sigmoid(pre)
    activation = (pre * sigma).astype(jnp.bfloat16)
    delta = (cotangent.astype(jnp.float32) * sigma * (1.0 + pre * (1.0 - sigma))).astype(
        jnp.bfloat16
    )
    delta_other = lax.ppermute(delta, "space", swap)
    delta_late, _ = lax.optimization_barrier((delta, delta_other))
    ahead = passed_along(lax.slice_in_dim(delta_late, 0, 2, axis=1), "group", -1)
    gwide = row_halo(jnp.concatenate([delta_late, ahead], axis=1), "space", 2)
    half = chans // 2
    both = jnp.concatenate([shifted, shifted_other], axis=0)
    both = lax.dynamic_slice_in_dim(both, lax.axis_index("space") * half, half, axis=4)
    both = jnp.pad(both, ((0, 0), (0, 0), (0, 0), (1, 1), (0, 0)))
    bstack = jnp.concatenate([both[:, :, :, b : b + cols] for b in range(3)], axis=4)
    bdelta = jnp.concatenate([delta, delta_other], axis=0)
    terms = []
    for k in range(3):
        masked = bdelta * same_fwd[k].astype(jnp.bfloat16)[:, :, None, None, None]
        for a in range(3):
            block = bstack[:, 2 - k : 2 - k + frames, a : a + rows]
            terms.append(
                jnp.einsum("sfhwk,sfhwc->kc", block, masked, preferred_element_type=jnp.float32)
            )
    total = jnp.stack(terms).reshape(27, half, chans)
    reduced = reduce_weight_grad(total)
    gwide = jnp.pad(gwide, ((0, 0), (0, 0), (0, 0), (1, 1), (0, 0)))
    gstack = jnp.concatenate([gwide[:, :, :, 2 - b : 2 - b + cols] for b in range(3)], axis=4)
    back = (
        weight.reshape(3, 3, 3, chans, chans)
        .transpose(0, 1, 2, 4, 3)
        .reshape(3, 3, 3 * chans, chans)
    )
    grad = jnp.zeros(video.shape, jnp.float32)
    for k in range(3):
        part = jnp.zeros(video.shape, jnp.float32)
        for a in range(3):
            block = gstack[:, k : k + frames, 2 - a : 2 - a + rows]
            part = part + jnp.einsum(
                "sfhwk,kc->sfhwc", block, back[k, a], preferred_element_type=jnp.float32
            )
        grad = grad + part * same_bwd[k].astype(jnp.float32)[:, :, None, None, None]
    return (activation, grad.astype(jnp.bfloat16), reduced)


def solution(mesh):
    placed = (
        P("dp", "group", "space", None, None),
        P("dp", "group", "space", None, None),
        P(),
        P("dp", "group"),
    )
    return jax.shard_map(
        local,
        mesh=mesh,
        in_specs=placed,
        out_specs=(
            P("dp", "group", "space", None, None),
            P("dp", "group", "space", None, None),
            P(None, ("group", "dp", "space")),
        ),
        check_vma=False,
    )
```

```python
import jax
import jax.numpy as jnp
from jax import lax
from jax.sharding import PartitionSpec as P


def passed_along(value, axis, by):
    length = lax.axis_size(axis)
    pairs = [(i, i + by) for i in range(length) if 0 <= i + by < length]
    return lax.ppermute(value, axis, pairs)


def row_halo(block, axis, dim):
    count = lax.axis_size(axis)
    forward = [(i, i + 1) for i in range(count - 1)]
    backward = [(target, source) for source, target in forward]
    low = lax.ppermute(
        lax.slice_in_dim(block, block.shape[dim] - 1, None, axis=dim), axis, forward
    )
    high = lax.ppermute(lax.slice_in_dim(block, 0, 1, axis=dim), axis, backward)
    return jnp.concatenate([low, block, high], axis=dim)


def halve(x, dim, axis, flip):
    size = x.shape[dim] // 2
    bit = (lax.axis_index(axis) // flip) % 2
    keep = lax.dynamic_slice_in_dim(x, bit * size, size, axis=dim)
    give = lax.dynamic_slice_in_dim(x, (1 - bit) * size, size, axis=dim)
    pairs = [(i, i ^ flip) for i in range(lax.axis_size(axis))]
    return keep + lax.ppermute(give, axis, pairs)


def quarter(x, dim, first, second):
    axis, high = first
    low = second[1]
    size = x.shape[dim] // 4
    where = lax.axis_index(axis)
    mine = ((where // high) % 2) * 2 + (where // low) % 2
    out = lax.dynamic_slice_in_dim(x, mine * size, size, axis=dim)
    for pattern, flip in ((2, high), (1, low), (3, high + low)):
        piece = lax.dynamic_slice_in_dim(x, jnp.bitwise_xor(mine, pattern) * size, size, axis=dim)
        pairs = [(i, i ^ flip) for i in range(lax.axis_size(axis))]
        out = out + lax.ppermute(piece, axis, pairs)
    return out


def bits_of(n):
    count = n.bit_length() - 1
    assert 1 << count == n
    return count


def owner_pairs(order, sizes):
    names = ("group", "dp", "space")
    count = sizes["group"] * sizes["dp"] * sizes["space"]
    pairs = []
    for linear in range(count):
        where = {
            "group": linear // (sizes["dp"] * sizes["space"]),
            "dp": (linear // sizes["space"]) % sizes["dp"],
            "space": linear % sizes["space"],
        }
        chunk = 0
        for axis, flip in order:
            chunk = chunk * 2 + (where[axis] // flip) % 2
        pairs.append((linear, chunk))
    return names, pairs


def reduce_weight_grad(total):
    ntaps, chans, outs = total.shape
    sizes = {name: lax.axis_size(name) for name in ("group", "dp", "space")}
    ng = sizes["group"]
    across = 4 if ng % 4 == 0 else ng
    down = ng // across
    assert chans * sizes["space"] == ng * sizes["dp"] * sizes["space"]
    first = ("space", 1)
    ys = [("group", across << b) for b in range(bits_of(down))]
    xs = [("group", 1 << b) for b in range(bits_of(across))]
    ds = [("dp", 1 << b) for b in range(bits_of(sizes["dp"]))]
    assert sizes["space"] == 2
    lanes = (ds, xs, ys)
    spread = [lane[0] for lane in lanes]
    rest = [key for lane in (xs, ys, ds) for key in lane[1:]]
    per = ntaps // len(lanes)
    parts, orders = [], []
    for n in range(len(lanes)):
        order = [first] + spread[n:] + spread[:n]
        part = total[n * per : (n + 1) * per]
        for axis, flip in order[1:]:
            part = halve(part, 1, axis, flip)
        parts.append(part)
        orders.append(order + rest)
    joined = jnp.stack(parts)
    steps = list(rest)
    while steps:
        if len(steps) > 1 and steps[0][0] == steps[1][0]:
            joined = quarter(joined, 2, steps[0], steps[1])
            steps = steps[2:]
        else:
            joined = halve(joined, 2, *steps[0])
            steps = steps[1:]
    parts = []
    for n, order in enumerate(orders):
        names, pairs = owner_pairs(order, sizes)
        parts.append(lax.ppermute(joined[n], names, pairs).reshape(per, outs))
    return jnp.concatenate(parts, axis=0)


def clip_tables(clip_id, frames):
    ids = lax.all_gather(clip_id, "group", axis=1, tiled=True)
    total = ids.shape[1]
    index = jnp.arange(total, dtype=jnp.int32)[None, :]
    prev = jnp.concatenate([jnp.full_like(ids[:, :1], -1), ids[:, :-1]], axis=1)
    boundary = ids != prev
    start = lax.cummax(jnp.where(boundary, index, 0), axis=1)
    position = index - start
    ext = jnp.concatenate([jnp.full_like(ids[:, :2], -1), ids], axis=1)
    same = jnp.stack([ext[:, 2 - k : 2 - k + total] == ids for k in range(3)], axis=0)
    first = lax.axis_index("group") * frames
    pos_pad = jnp.concatenate([jnp.zeros_like(position[:, :2]), position], axis=1)
    pos_wide = lax.dynamic_slice_in_dim(pos_pad, first, frames + 2, axis=1)
    same_pad = jnp.concatenate([same, jnp.zeros_like(same[:, :, :2])], axis=2)
    own = lax.dynamic_slice_in_dim(same_pad, first, frames + 2, axis=2)
    fwd = own[:, :, :frames]
    bwd = jnp.stack([own[k, :, k : k + frames] for k in range(3)], axis=0)
    return pos_wide, fwd, bwd


def local(video, cotangent, weight, clip_id):
    frames = video.shape[1]
    rows = video.shape[2]
    cols = video.shape[3]
    chans = video.shape[4]
    assert lax.axis_size("space") == 2
    swap = [(0, 1), (1, 0)]
    where_s = lax.axis_index("space")
    tail = lax.slice_in_dim(video, frames - 2, None, axis=1)
    past = passed_along(tail, "group", 1)
    other_now = lax.ppermute(video, "space", swap)
    count = lax.axis_size("group")
    diagonal = [(g * 2 + c, (g + 1) * 2 + 1 - c) for g in range(count - 1) for c in range(2)]
    other_past = lax.ppermute(tail, ("group", "space"), diagonal)
    mine = jnp.concatenate([past, video], axis=1)
    theirs = jnp.concatenate([other_past, other_now], axis=1)
    full = jnp.where(
        where_s == 0,
        jnp.concatenate([mine, theirs], axis=2),
        jnp.concatenate([theirs, mine], axis=2),
    )
    pos_wide, same_fwd, same_bwd = clip_tables(clip_id, frames)
    omega = 0.37 * (jnp.arange(chans) % 8 + 1).astype(jnp.float32)
    embed = jnp.sin(pos_wide.astype(jnp.float32)[:, :, None] * omega)
    whole = (full.astype(jnp.float32) + embed[:, :, None, None, :]).astype(jnp.bfloat16)
    whole = jnp.pad(whole, ((0, 0), (0, 0), (1, 1), (0, 0), (0, 0)))
    shifted = lax.dynamic_slice_in_dim(whole, where_s * rows, rows + 2, axis=2)
    shifted_other = lax.dynamic_slice_in_dim(whole, (1 - where_s) * rows, rows + 2, axis=2)
    maskf = same_fwd.astype(jnp.float32)
    widened = jnp.pad(shifted, ((0, 0), (0, 0), (0, 0), (1, 1), (0, 0)))
    stacked = jnp.concatenate([widened[:, :, :, b : b + cols] for b in range(3)], axis=4)
    taps = weight.reshape(3, 3, 3 * chans, chans)
    pre = jnp.zeros(video.shape, jnp.float32)
    for k in range(3):
        part = jnp.zeros(video.shape, jnp.float32)
        for a in range(3):
            block = stacked[:, 2 - k : 2 - k + frames, a : a + rows]
            part = part + jnp.einsum(
                "sfhwk,kc->sfhwc", block, taps[k, a], preferred_element_type=jnp.float32
            )
        pre = pre + part * maskf[k][:, :, None, None, None]
    sigma = jax.nn.sigmoid(pre)
    activation = (pre * sigma).astype(jnp.bfloat16)
    delta = (cotangent.astype(jnp.float32) * sigma * (1.0 + pre * (1.0 - sigma))).astype(
        jnp.bfloat16
    )
    delta_other = lax.ppermute(delta, "space", swap)
    delta_late, _ = lax.optimization_barrier((delta, delta_other))
    ahead = passed_along(lax.slice_in_dim(delta_late, 0, 2, axis=1), "group", -1)
    gwide = row_halo(jnp.concatenate([delta_late, ahead], axis=1), "space", 2)
    half = chans // 2
    both = jnp.concatenate([shifted, shifted_other], axis=0)
    both = lax.dynamic_slice_in_dim(both, lax.axis_index("space") * half, half, axis=4)
    both = jnp.pad(both, ((0, 0), (0, 0), (0, 0), (1, 1), (0, 0)))
    bstack = jnp.concatenate([both[:, :, :, b : b + cols] for b in range(3)], axis=4)
    bdelta = jnp.concatenate([delta, delta_other], axis=0)
    terms = []
    for k in range(3):
        masked = bdelta * same_fwd[k].astype(jnp.bfloat16)[:, :, None, None, None]
        for a in range(3):
            block = bstack[:, 2 - k : 2 - k + frames, a : a + rows]
            terms.append(
                jnp.einsum("sfhwk,sfhwc->kc", block, masked, preferred_element_type=jnp.float32)
            )
    total = jnp.stack(terms).reshape(27, half, chans)
    reduced = reduce_weight_grad(total)
    gwide = jnp.pad(gwide, ((0, 0), (0, 0), (0, 0), (1, 1), (0, 0)))
    gstack = jnp.concatenate([gwide[:, :, :, 2 - b : 2 - b + cols] for b in range(3)], axis=4)
    back = (
        weight.reshape(3, 3, 3, chans, chans)
        .transpose(0, 1, 2, 4, 3)
        .reshape(3, 3, 3 * chans, chans)
    )
    grad = jnp.zeros(video.shape, jnp.float32)
    for k in range(3):
        part = jnp.zeros(video.shape, jnp.float32)
        for a in range(3):
            block = gstack[:, k : k + frames, 2 - a : 2 - a + rows]
            part = part + jnp.einsum(
                "sfhwk,kc->sfhwc", block, back[k, a], preferred_element_type=jnp.float32
            )
        grad = grad + part * same_bwd[k].astype(jnp.float32)[:, :, None, None, None]
    return (activation, grad.astype(jnp.bfloat16), reduced)


def solution(mesh):
    placed = (
        P("dp", "group", "space", None, None),
        P("dp", "group", "space", None, None),
        P(),
        P("dp", "group"),
    )
    return jax.shard_map(
        local,
        mesh=mesh,
        in_specs=placed,
        out_specs=(
            P("dp", "group", "space", None, None),
            P("dp", "group", "space", None, None),
            P(None, ("group", "dp", "space")),
        ),
        check_vma=False,
    )
```

```python
import jax
import jax.numpy as jnp
from jax import lax
from jax.sharding import PartitionSpec as P


def passed_along(value, axis, by):
    length = lax.axis_size(axis)
    pairs = [(i, i + by) for i in range(length) if 0 <= i + by < length]
    return lax.ppermute(value, axis, pairs)


def row_halo(block, axis, dim):
    count = lax.axis_size(axis)
    forward = [(i, i + 1) for i in range(count - 1)]
    backward = [(target, source) for source, target in forward]
    low = lax.ppermute(
        lax.slice_in_dim(block, block.shape[dim] - 1, None, axis=dim), axis, forward
    )
    high = lax.ppermute(lax.slice_in_dim(block, 0, 1, axis=dim), axis, backward)
    return jnp.concatenate([low, block, high], axis=dim)


def halve(x, dim, axis, flip):
    size = x.shape[dim] // 2
    bit = (lax.axis_index(axis) // flip) % 2
    keep = lax.dynamic_slice_in_dim(x, bit * size, size, axis=dim)
    give = lax.dynamic_slice_in_dim(x, (1 - bit) * size, size, axis=dim)
    pairs = [(i, i ^ flip) for i in range(lax.axis_size(axis))]
    return keep + lax.ppermute(give, axis, pairs)


def quarter(x, dim, first, second):
    axis, high = first
    low = second[1]
    size = x.shape[dim] // 4
    where = lax.axis_index(axis)
    mine = ((where // high) % 2) * 2 + (where // low) % 2
    out = lax.dynamic_slice_in_dim(x, mine * size, size, axis=dim)
    for pattern, flip in ((2, high), (1, low), (3, high + low)):
        piece = lax.dynamic_slice_in_dim(x, jnp.bitwise_xor(mine, pattern) * size, size, axis=dim)
        pairs = [(i, i ^ flip) for i in range(lax.axis_size(axis))]
        out = out + lax.ppermute(piece, axis, pairs)
    return out


def bits_of(n):
    count = n.bit_length() - 1
    assert 1 << count == n
    return count


def owner_pairs(order, sizes):
    names = ("group", "dp", "space")
    count = sizes["group"] * sizes["dp"] * sizes["space"]
    pairs = []
    for linear in range(count):
        where = {
            "group": linear // (sizes["dp"] * sizes["space"]),
            "dp": (linear // sizes["space"]) % sizes["dp"],
            "space": linear % sizes["space"],
        }
        chunk = 0
        for axis, flip in order:
            chunk = chunk * 2 + (where[axis] // flip) % 2
        pairs.append((linear, chunk))
    return names, pairs


def reduce_weight_grad(total):
    ntaps, chans, outs = total.shape
    sizes = {name: lax.axis_size(name) for name in ("group", "dp", "space")}
    ng = sizes["group"]
    across = 4 if ng % 4 == 0 else ng
    down = ng // across
    assert chans * sizes["space"] == ng * sizes["dp"] * sizes["space"]
    first = ("space", 1)
    ys = [("group", across << b) for b in range(bits_of(down))]
    xs = [("group", 1 << b) for b in range(bits_of(across))]
    ds = [("dp", 1 << b) for b in range(bits_of(sizes["dp"]))]
    assert sizes["space"] == 2
    lanes = (ds, xs, ys)
    spread = [lane[0] for lane in lanes]
    rest = [key for lane in (xs, ys, ds) for key in lane[1:]]
    per = ntaps // len(lanes)
    parts, orders = [], []
    for n in range(len(lanes)):
        order = [first] + [spread[0], spread[1], spread[2]][n:] + spread[:n]
        if n == 2:
            order = [first, spread[2], spread[1], spread[0]]
        part = total[n * per : (n + 1) * per]
        steps = order[1:]
        while steps:
            if len(steps) > 1 and steps[0][0] == steps[1][0]:
                part = quarter(part, 1, steps[0], steps[1])
                steps = steps[2:]
            else:
                part = halve(part, 1, *steps[0])
                steps = steps[1:]
        parts.append(part)
        orders.append(order + rest)
    joined = jnp.stack(parts)
    steps = list(rest)
    while steps:
        if len(steps) > 1 and steps[0][0] == steps[1][0]:
            joined = quarter(joined, 2, steps[0], steps[1])
            steps = steps[2:]
        else:
            joined = halve(joined, 2, *steps[0])
            steps = steps[1:]
    parts = []
    for n, order in enumerate(orders):
        names, pairs = owner_pairs(order, sizes)
        parts.append(lax.ppermute(joined[n], names, pairs).reshape(per, outs))
    return jnp.concatenate(parts, axis=0)


def clip_tables(clip_id, frames):
    ids = lax.all_gather(clip_id, "group", axis=1, tiled=True)
    total = ids.shape[1]
    index = jnp.arange(total, dtype=jnp.int32)[None, :]
    prev = jnp.concatenate([jnp.full_like(ids[:, :1], -1), ids[:, :-1]], axis=1)
    boundary = ids != prev
    start = lax.cummax(jnp.where(boundary, index, 0), axis=1)
    position = index - start
    ext = jnp.concatenate([jnp.full_like(ids[:, :2], -1), ids], axis=1)
    same = jnp.stack([ext[:, 2 - k : 2 - k + total] == ids for k in range(3)], axis=0)
    first = lax.axis_index("group") * frames
    pos_pad = jnp.concatenate([jnp.zeros_like(position[:, :2]), position], axis=1)
    pos_wide = lax.dynamic_slice_in_dim(pos_pad, first, frames + 2, axis=1)
    same_pad = jnp.concatenate([same, jnp.zeros_like(same[:, :, :2])], axis=2)
    own = lax.dynamic_slice_in_dim(same_pad, first, frames + 2, axis=2)
    fwd = own[:, :, :frames]
    bwd = jnp.stack([own[k, :, k : k + frames] for k in range(3)], axis=0)
    return pos_wide, fwd, bwd


def local(video, cotangent, weight, clip_id):
    frames = video.shape[1]
    rows = video.shape[2]
    cols = video.shape[3]
    chans = video.shape[4]
    assert lax.axis_size("space") == 2
    swap = [(0, 1), (1, 0)]
    where_s = lax.axis_index("space")
    tail = lax.slice_in_dim(video, frames - 2, None, axis=1)
    past = passed_along(tail, "group", 1)
    other_now = lax.ppermute(video, "space", swap)
    count = lax.axis_size("group")
    diagonal = [(g * 2 + c, (g + 1) * 2 + 1 - c) for g in range(count - 1) for c in range(2)]
    other_past = lax.ppermute(tail, ("group", "space"), diagonal)
    mine = jnp.concatenate([past, video], axis=1)
    theirs = jnp.concatenate([other_past, other_now], axis=1)
    full = jnp.where(
        where_s == 0,
        jnp.concatenate([mine, theirs], axis=2),
        jnp.concatenate([theirs, mine], axis=2),
    )
    pos_wide, same_fwd, same_bwd = clip_tables(clip_id, frames)
    omega = 0.37 * (jnp.arange(chans) % 8 + 1).astype(jnp.float32)
    embed = jnp.sin(pos_wide.astype(jnp.float32)[:, :, None] * omega)
    whole = (full.astype(jnp.float32) + embed[:, :, None, None, :]).astype(jnp.bfloat16)
    whole = jnp.pad(whole, ((0, 0), (0, 0), (1, 1), (0, 0), (0, 0)))
    shifted = lax.dynamic_slice_in_dim(whole, where_s * rows, rows + 2, axis=2)
    shifted_other = lax.dynamic_slice_in_dim(whole, (1 - where_s) * rows, rows + 2, axis=2)
    maskf = same_fwd.astype(jnp.float32)
    widened = jnp.pad(shifted, ((0, 0), (0, 0), (0, 0), (1, 1), (0, 0)))
    stacked = jnp.concatenate([widened[:, :, :, b : b + cols] for b in range(3)], axis=4)
    taps = weight.reshape(3, 3, 3 * chans, chans)
    pre = jnp.zeros(video.shape, jnp.float32)
    for k in range(3):
        part = jnp.zeros(video.shape, jnp.float32)
        for a in range(3):
            block = stacked[:, 2 - k : 2 - k + frames, a : a + rows]
            part = part + jnp.einsum(
                "sfhwk,kc->sfhwc", block, taps[k, a], preferred_element_type=jnp.float32
            )
        pre = pre + part * maskf[k][:, :, None, None, None]
    sigma = jax.nn.sigmoid(pre)
    activation = (pre * sigma).astype(jnp.bfloat16)
    delta = (cotangent.astype(jnp.float32) * sigma * (1.0 + pre * (1.0 - sigma))).astype(
        jnp.bfloat16
    )
    delta_other = lax.ppermute(delta, "space", swap)
    delta_late, _ = lax.optimization_barrier((delta, delta_other))
    ahead = passed_along(lax.slice_in_dim(delta_late, 0, 2, axis=1), "group", -1)
    gwide = row_halo(jnp.concatenate([delta_late, ahead], axis=1), "space", 2)
    half = chans // 2
    both = jnp.concatenate([shifted, shifted_other], axis=0)
    both = lax.dynamic_slice_in_dim(both, lax.axis_index("space") * half, half, axis=4)
    both = jnp.pad(both, ((0, 0), (0, 0), (0, 0), (1, 1), (0, 0)))
    bstack = jnp.concatenate([both[:, :, :, b : b + cols] for b in range(3)], axis=4)
    bdelta = jnp.concatenate([delta, delta_other], axis=0)
    terms = []
    for k in range(3):
        masked = bdelta * same_fwd[k].astype(jnp.bfloat16)[:, :, None, None, None]
        for a in range(3):
            block = bstack[:, 2 - k : 2 - k + frames, a : a + rows]
            terms.append(
                jnp.einsum("sfhwk,sfhwc->kc", block, masked, preferred_element_type=jnp.float32)
            )
    total = jnp.stack(terms).reshape(27, half, chans)
    reduced = reduce_weight_grad(total)
    gwide = jnp.pad(gwide, ((0, 0), (0, 0), (0, 0), (1, 1), (0, 0)))
    gstack = jnp.concatenate([gwide[:, :, :, 2 - b : 2 - b + cols] for b in range(3)], axis=4)
    back = (
        weight.reshape(3, 3, 3, chans, chans)
        .transpose(0, 1, 2, 4, 3)
        .reshape(3, 3, 3 * chans, chans)
    )
    grad = jnp.zeros(video.shape, jnp.float32)
    for k in range(3):
        part = jnp.zeros(video.shape, jnp.float32)
        for a in range(3):
            block = gstack[:, k : k + frames, 2 - a : 2 - a + rows]
            part = part + jnp.einsum(
                "sfhwk,kc->sfhwc", block, back[k, a], preferred_element_type=jnp.float32
            )
        grad = grad + part * same_bwd[k].astype(jnp.float32)[:, :, None, None, None]
    return (activation, grad.astype(jnp.bfloat16), reduced)


def solution(mesh):
    placed = (
        P("dp", "group", "space", None, None),
        P("dp", "group", "space", None, None),
        P(),
        P("dp", "group"),
    )
    return jax.shard_map(
        local,
        mesh=mesh,
        in_specs=placed,
        out_specs=(
            P("dp", "group", "space", None, None),
            P("dp", "group", "space", None, None),
            P(None, ("group", "dp", "space")),
        ),
        check_vma=False,
    )
```
